256 devices in a mesh: date: 2 (over z_hi), strip: 128 (over z_lo, y, x, core).
Axes of the slice: x: 4, y: 4, z: 8 (z_hi: 2, z_lo: 4; z = z_hi * 4 + z_lo), core: 2. Of those that a mesh axis runs over, the one named last changes fastest.
Arguments:
- raw_echoes: bfloat16 [2, 4, 8192, 1024], P(None, 'date', 'strip'), may hold values from -6 to 6
- range_phase: float32 [1024], replicated, may hold values from -3.140625 to 3.140625
- azimuth_phase: float32 [8192], replicated, may hold values from -3.140625 to 3.140625
- calibration: float32 [4, 1024], P(None, ('date', 'strip')), may hold values from 1 to 10
Outputs:
- linked: float32 [2, 4, 1024, 8192], P(None, None, ('date', 'strip'))
- quality: float32 [1024, 8192], P(('date', 'strip'))
The draws below stay inside these ranges and needn't reach their ends.
All inputs are finite; a program needn't handle non-finite values.
Results may differ from the reference program's by a relative error of at most 0.0003.
Values may be sent and summed in bfloat16 or wider, within the bound.
No kernel may reach another device: no remote copies, remote signals or barrier semaphores. Data moves between devices by JAX's collectives and lax.ppermute only.
A program may use at most 64 MiB of HBM per device.

```python
import math
import jax
import jax.numpy as jnp
from jax import lax

LINES = 8192
RANGE = 1024
WIN_HALF = 11
POWER_ITERS = 6
SMOOTH_PASSES = 2
DATES = 4


def block_scale(rng, dims, split, smallest, high):
    level = 1.0
    for dim, parts in split:
        steps = jax.random.uniform(jax.random.fold_in(jax.random.fold_in(rng, 6), dim), (parts,), jnp.float32, smallest / len(split), high / len(split))
        level = level * jnp.repeat(jnp.exp(steps), dims[dim] // parts).reshape((-1,) + (1,) * (len(dims) - 1 - dim))
    return level


def scatter_about(key, dims, spread, bound, pieces=(), kind=jnp.bfloat16):
    result = spread * jax.random.normal(key, dims, jnp.float32)
    if pieces:
        result = result * block_scale(key, dims, pieces, -0.22, 0.18)
    return jnp.clip(result, -bound, bound).astype(kind)


def setup_inputs(seed: int = 0) -> dict:
    arg_keys = jax.random.split(jax.random.key(seed), 5)
    return {
        "raw_echoes": scatter_about(arg_keys[0], (2, DATES, LINES, RANGE), 1.0, 6.0, ((1, 2), (2, 128))),
        "range_phase": jnp.clip(jax.random.uniform(arg_keys[1], (RANGE,), jnp.float32, -3.140625, 3.140625), -3.140625, 3.140625),
        "azimuth_phase": jnp.clip(jax.random.uniform(arg_keys[2], (LINES,), jnp.float32, -3.140625, 3.140625), -3.140625, 3.140625),
        "calibration": jnp.clip(jnp.exp(math.log(10.0) - 2.3025851 * jax.random.uniform(arg_keys[3], (DATES, RANGE), jnp.float32) ** block_scale(arg_keys[3], (DATES, RANGE), ((1, 256),), -0.2, 0.2)), 1.0, 10.0),
    }


def running_window(values):
    width = 2 * WIN_HALF + 1
    count = values.shape[-1]
    level = jnp.pad(values, ((0, 0), (0, 0), (WIN_HALF, WIN_HALF)))
    total = jnp.zeros_like(values)
    offset = 0
    span = 1
    while span <= width:
        if width & span:
            total = total + level[..., offset:offset + count]
            offset = offset + span
        level = level[..., :-span] + level[..., span:]
        span = span * 2
    return total

def link_block(real_ext, imag_ext, valid_mask):
    date_count = real_ext.shape[0]
    pair_list = [(former, latter) for former in range(date_count) for latter in range(former + 1, date_count)]
    terms = [real_ext[former] * real_ext[former] + imag_ext[former] * imag_ext[former] for former in range(date_count)]
    for former, latter in pair_list:
        terms.append(real_ext[former] * real_ext[latter] + imag_ext[former] * imag_ext[latter])
        terms.append(imag_ext[former] * real_ext[latter] - real_ext[former] * imag_ext[latter])
    stacked = jnp.stack(terms)
    across = stacked[:, :-2] + stacked[:, 1:-1] + stacked[:, 2:]
    window = running_window(across)
    window = window / (3 * (2 * WIN_HALF + 1))
    powers = window[:date_count] + 1e-06
    coherence = {}
    for number, pair in enumerate(pair_list):
        factor = lax.rsqrt(powers[pair[0]] * powers[pair[1]])
        coherence[pair] = (window[date_count + 2 * number] * factor, window[date_count + 2 * number + 1] * factor)
    vector_real = [jnp.ones_like(powers[0]) for former in range(date_count)]
    vector_imag = [jnp.zeros_like(powers[0]) for former in range(date_count)]
    for iteration in range(POWER_ITERS):
        new_real = []
        new_imag = []
        for target in range(date_count):
            acc_real = vector_real[target]
            acc_imag = vector_imag[target]
            for source in range(date_count):
                if source != target:
                    if target < source:
                        part_real, part_imag = coherence[target, source]
                    else:
                        part_real, part_imag = coherence[source, target]
                        part_imag = -part_imag
                    acc_real = acc_real + part_real * vector_real[source] - part_imag * vector_imag[source]
                    acc_imag = acc_imag + part_real * vector_imag[source] + part_imag * vector_real[source]
            new_real.append(acc_real)
            new_imag.append(acc_imag)
        mean_square = sum((new_real[target] * new_real[target] + new_imag[target] * new_imag[target] for target in range(date_count))) / date_count
        factor = lax.rsqrt(jnp.maximum(mean_square, 1.0))
        vector_real = [entry * factor for entry in new_real]
        vector_imag = [entry * factor for entry in new_imag]
    magnitude = sum((jnp.sqrt(coherence[pair][0] * coherence[pair][0] + coherence[pair][1] * coherence[pair][1]) for pair in pair_list)) / len(pair_list)
    quality = valid_mask[:, None] * (0.05 + magnitude)
    vector = jnp.stack([jnp.stack(vector_real), jnp.stack(vector_imag)])
    return (vector, quality)

def smooth_once(vector, quality):
    weighted = vector * quality
    numerator = weighted[:, :, :-2] + weighted[:, :, 1:-1] + weighted[:, :, 2:]
    denominator = quality[:-2] + quality[1:-1] + quality[2:]
    denominator = jnp.where(denominator > 0, denominator, 1.0)
    return (numerator / denominator, quality[1:-1])

def reference(raw_echoes, range_phase, azimuth_phase, calibration):
    samples = raw_echoes[0].astype(jnp.float32) + 1j * raw_echoes[1].astype(jnp.float32)
    ranged = jnp.fft.ifft(jnp.fft.fft(samples, axis=2) * jnp.exp(1j * range_phase)[None, None, :], axis=2)
    focused = jnp.fft.ifft(jnp.fft.fft(ranged, axis=1) * jnp.exp(1j * azimuth_phase)[None, :, None], axis=1)
    image = jnp.swapaxes(focused, 1, 2) * calibration[:, :, None]
    margin = 1 + SMOOTH_PASSES
    padded_real = jnp.pad(jnp.real(image), ((0, 0), (margin, margin), (0, 0)))
    padded_imag = jnp.pad(jnp.imag(image), ((0, 0), (margin, margin), (0, 0)))
    block_size = 64

    def one_block(position):
        start = position * block_size
        slab_real = lax.dynamic_slice_in_dim(padded_real, start, block_size + 2 * margin, 1)
        slab_imag = lax.dynamic_slice_in_dim(padded_imag, start, block_size + 2 * margin, 1)
        columns = start - SMOOTH_PASSES + jnp.arange(block_size + 2 * SMOOTH_PASSES, dtype=jnp.int32)
        valid_mask = ((columns >= 0) & (columns < RANGE)).astype(slab_real.dtype)
        vector, quality = link_block(slab_real, slab_imag, valid_mask)
        for passes in range(SMOOTH_PASSES):
            vector, quality = smooth_once(vector, quality)
        return (vector, quality)
    positions = jnp.arange(RANGE // block_size, dtype=jnp.int32)
    vectors, qualities = lax.map(one_block, positions)
    linked = jnp.moveaxis(vectors, 0, 2).reshape(2, DATES, RANGE, LINES)
    quality = qualities.reshape(RANGE, LINES)
    return (linked, quality)
```

```python
import math

import jax
import jax.numpy as jnp
from jax import lax
from jax.sharding import PartitionSpec as P

WIN_HALF = 11
POWER_ITERS = 6
SMOOTH_PASSES = 2


HIGHEST = lax.Precision.HIGHEST


def split_up(x, dim, count):
    shape = x.shape
    tiles = x.reshape(*shape[:dim], count, shape[dim] // count, *shape[dim + 1 :])
    return jnp.moveaxis(tiles, dim, 0)


def laid_out(tiles, dim):
    shape = list(tiles.shape[1:])
    shape[dim] *= tiles.shape[0]
    return jnp.moveaxis(tiles, 0, dim).reshape(shape)


def one_exchange(x, axis, axes, splits, concats):
    sizes = [lax.axis_size(a) for a in axes]
    tiles = split_up(x, splits[0], sizes[0])
    tiles = jnp.moveaxis(split_up(tiles, splits[1] + 1, sizes[1]), 0, 1)
    inside = tiles.shape[2:]
    tiles = tiles.reshape(-1, *inside)
    tiles = lax.all_to_all(tiles, axis, split_axis=0, concat_axis=0, tiled=True)
    tiles = laid_out(tiles.reshape(*sizes, *inside), concats[0] + 1)
    return laid_out(tiles, concats[1])


def extended_2(x, sides, width):
    edges = {}
    for axis, dim in sides:
        count, length = (lax.axis_size(axis), x.shape[dim])
        up = [(i, (i + 1) % count) for i in range(count - 1)]
        last = lax.slice_in_dim(x, length - width, length, axis=dim)
        first = lax.slice_in_dim(x, 0, width, axis=dim)
        edges[dim] = (
            lax.ppermute(last, axis, up),
            lax.ppermute(first, axis, [(b, a) for a, b in up]),
        )
    done = []
    for _, dim in sides:
        low, high = edges[dim]
        around = [(width, width) if d in done else (0, 0) for d in range(x.ndim)]
        x = jnp.concatenate([jnp.pad(low, around), x, jnp.pad(high, around)], axis=dim)
        done.append(dim)
    return x


def dft_table(length, direction):
    counter = jnp.arange(length, dtype=jnp.int32)
    product = counter[:, None] * counter[None, :] % length
    angles = product.astype(jnp.float32) * (direction * 2.0 * math.pi / length)
    cosine = jnp.cos(angles)
    sine_part = jnp.sin(angles)
    return jnp.stack([jnp.stack([cosine, -sine_part]), jnp.stack([sine_part, cosine])])


def twiddle(outer_size, inner_size, direction):
    product = (
        jnp.arange(outer_size, dtype=jnp.int32)[:, None]
        * jnp.arange(inner_size, dtype=jnp.int32)[None, :]
        % (outer_size * inner_size)
    )
    angles = product.astype(jnp.float32) * (direction * 2.0 * math.pi / (outer_size * inner_size))
    return (jnp.cos(angles), jnp.sin(angles))


def rotate(values, cosine, sine_part):
    return jnp.stack(
        [values[0] * cosine - values[1] * sine_part, values[0] * sine_part + values[1] * cosine]
    )


def spectral_core(values, phases):
    outer_size = values.shape[-2]
    inner_size = values.shape[-1]
    values = jnp.einsum("pqkn,q...nm->p...km", dft_table(outer_size, -1), values, precision=HIGHEST)
    cos_part, sin_part = twiddle(outer_size, inner_size, -1)
    values = rotate(values, cos_part, sin_part)
    values = jnp.einsum("pqjm,q...km->p...kj", dft_table(inner_size, -1), values, precision=HIGHEST)
    phase_grid = phases.reshape(inner_size, outer_size).T
    values = rotate(values, jnp.cos(phase_grid), jnp.sin(phase_grid))
    values = jnp.einsum("pqmj,q...kj->p...km", dft_table(inner_size, 1), values, precision=HIGHEST)
    cos_part, sin_part = twiddle(outer_size, inner_size, 1)
    return rotate(values, cos_part, sin_part)


def azimuth_compress(values, phases):
    length = values.shape[-1]
    inner_size = 128
    outer_size = length // inner_size
    spectrum = spectral_core(values.reshape(values.shape[:-1] + (outer_size, inner_size)), phases)
    result = (
        jnp.einsum("pqnk,q...km->p...nm", dft_table(outer_size, 1), spectrum, precision=HIGHEST)
        / length
    )
    return result.reshape(values.shape)


def range_compress(values, phases, row_count):
    length = values.shape[-1]
    inner_size = 128
    outer_size = length // inner_size
    spectrum = spectral_core(values.reshape(values.shape[:-1] + (outer_size, inner_size)), phases)
    inverse_rows = dft_table(outer_size, 1)
    result = jnp.einsum("pqnk,qdlkm->pdnml", inverse_rows, spectrum, precision=HIGHEST) / length
    return result.reshape(2, values.shape[1], row_count * inner_size, values.shape[2])


def running_window(values):
    width = 2 * WIN_HALF + 1
    count = values.shape[-1]
    level = jnp.pad(values, ((0, 0), (0, 0), (WIN_HALF, WIN_HALF)))
    total = jnp.zeros_like(values)
    offset = 0
    span = 1
    while span <= width:
        if width & span:
            total = total + level[..., offset : offset + count]
            offset = offset + span
        level = level[..., :-span] + level[..., span:]
        span = span * 2
    return total


def link_block(real_ext, imag_ext, valid_mask):
    date_count = real_ext.shape[0]
    pair_list = [
        (former, latter) for former in range(date_count) for latter in range(former + 1, date_count)
    ]
    terms = [
        real_ext[former] * real_ext[former] + imag_ext[former] * imag_ext[former]
        for former in range(date_count)
    ]
    for former, latter in pair_list:
        terms.append(real_ext[former] * real_ext[latter] + imag_ext[former] * imag_ext[latter])
        terms.append(imag_ext[former] * real_ext[latter] - real_ext[former] * imag_ext[latter])
    stacked = jnp.stack(terms)
    across = stacked[:, :-2] + stacked[:, 1:-1] + stacked[:, 2:]
    window = running_window(across)
    window = window / (3 * (2 * WIN_HALF + 1))
    powers = window[:date_count] + 1e-06
    coherence = {}
    for number, pair in enumerate(pair_list):
        factor = lax.rsqrt(powers[pair[0]] * powers[pair[1]])
        coherence[pair] = (
            window[date_count + 2 * number] * factor,
            window[date_count + 2 * number + 1] * factor,
        )
    vector_real = [jnp.ones_like(powers[0]) for former in range(date_count)]
    vector_imag = [jnp.zeros_like(powers[0]) for former in range(date_count)]
    for iteration in range(POWER_ITERS):
        new_real = []
        new_imag = []
        for target in range(date_count):
            acc_real = vector_real[target]
            acc_imag = vector_imag[target]
            for source in range(date_count):
                if source != target:
                    if target < source:
                        part_real, part_imag = coherence[target, source]
                    else:
                        part_real, part_imag = coherence[source, target]
                        part_imag = -part_imag
                    acc_real = (
                        acc_real + part_real * vector_real[source] - part_imag * vector_imag[source]
                    )
                    acc_imag = (
                        acc_imag + part_real * vector_imag[source] + part_imag * vector_real[source]
                    )
            new_real.append(acc_real)
            new_imag.append(acc_imag)
        mean_square = (
            sum(
                (
                    new_real[target] * new_real[target] + new_imag[target] * new_imag[target]
                    for target in range(date_count)
                )
            )
            / date_count
        )
        factor = lax.rsqrt(jnp.maximum(mean_square, 1.0))
        vector_real = [entry * factor for entry in new_real]
        vector_imag = [entry * factor for entry in new_imag]
    magnitude = sum(
        (
            jnp.sqrt(
                coherence[pair][0] * coherence[pair][0] + coherence[pair][1] * coherence[pair][1]
            )
            for pair in pair_list
        )
    ) / len(pair_list)
    quality = valid_mask[:, None] * (0.05 + magnitude)
    vector = jnp.stack([jnp.stack(vector_real), jnp.stack(vector_imag)])
    return (vector, quality)


def shards(raw_echoes, range_phase, azimuth_phase, calibration):
    groups = lax.axis_size("date")
    group_dates = raw_echoes.shape[1]
    local_lines = raw_echoes.shape[2]
    length = raw_echoes.shape[3]
    outer_size = length // 128
    ranged = range_compress(raw_echoes.astype(jnp.float32), range_phase, outer_size)
    ranged = ranged.reshape(2, group_dates, groups, length // groups, local_lines)
    turned = one_exchange(ranged, ("date", "strip"), ("date", "strip"), (2, 3), (1, 4))
    focused = azimuth_compress(turned, azimuth_phase)
    all_dates = group_dates * groups
    column_count = calibration.shape[1]
    line_count = focused.shape[-1]
    image = focused.reshape(2, all_dates, column_count, line_count) * calibration[None, :, :, None]
    halo = 1 + SMOOTH_PASSES
    extended = extended_2(image, ((("date", "strip"), 2),), halo)
    total_columns = column_count * lax.axis_size("date") * lax.axis_size("strip")
    first = lax.axis_index(("date", "strip")) * column_count - SMOOTH_PASSES
    columns = first + jnp.arange(column_count + 2 * SMOOTH_PASSES, dtype=jnp.int32)
    valid_mask = ((columns >= 0) & (columns < total_columns)).astype(jnp.float32)
    vector, quality = link_block(extended[0], extended[1], valid_mask)
    for passes in range(SMOOTH_PASSES):
        weighted = vector * quality
        numerator = weighted[:, :, :-2] + weighted[:, :, 1:-1] + weighted[:, :, 2:]
        denominator = quality[:-2] + quality[1:-1] + quality[2:]
        denominator = jnp.where(denominator > 0, denominator, 1.0)
        vector = numerator / denominator
        quality = quality[1:-1]
    return (vector, quality)


def solution(mesh):
    in_specs = (P(None, "date", "strip", None), P(), P(), P(None, ("date", "strip")))
    out_specs = (P(None, None, ("date", "strip"), None), P(("date", "strip"), None))
    return jax.shard_map(shards, mesh=mesh, in_specs=in_specs, out_specs=out_specs, check_vma=False)
```

```python
import math

import jax
import jax.numpy as jnp
from jax import lax
from jax.experimental import pallas as pl
from jax.experimental.pallas import tpu as pltpu
from jax.sharding import PartitionSpec as P

WIN_HALF = 11
POWER_ITERS = 6
SMOOTH_PASSES = 2


HIGHEST = lax.Precision.HIGHEST
BLOCK = 512
EDGE = 128
CHUNK = 128


def window_lines(values):
    ones = values + pltpu.roll(values, 1, 1)
    twos = ones + pltpu.roll(ones, 2, 1)
    fours = twos + pltpu.roll(twos, 4, 1)
    eights = fours + pltpu.roll(fours, 8, 1)
    width = values.shape[1]
    return (
        pltpu.roll(eights, width - WIN_HALF, 1)
        + pltpu.roll(twos, 5, 1)
        + pltpu.roll(ones, 9, 1)
        + pltpu.roll(values, WIN_HALF, 1)
    )


def link_kernel(mask_ref, prev_ref, cur_ref, next_ref, vec_ref, qual_ref, image, sums):
    step = pl.program_id(0)
    last = pl.num_programs(0) - 1
    dates = cur_ref.shape[1]
    block = cur_ref.shape[3]
    image[:, :, :, EDGE : EDGE + block] = cur_ref[...]
    image[:, :, :, :EDGE] = jnp.where(step > 0, prev_ref[...], 0.0)
    image[:, :, :, EDGE + block :] = jnp.where(step < last, next_ref[...], 0.0)
    rows = sums.shape[1]
    pairs = [(a, b) for a in range(dates) for b in range(a + 1, dates)]

    def part(p, d, shift):
        return image[p, d, pl.ds(shift, rows), :]

    def term(kind, a, b, shift):
        ra, ia = part(0, a, shift), part(1, a, shift)
        if kind == 0:
            return ra * ra + ia * ia
        rb, ib = part(0, b, shift), part(1, b, shift)
        if kind == 1:
            return ra * rb + ia * ib
        return ia * rb - ra * ib

    specs = [(0, a, a) for a in range(dates)]
    for a, b in pairs:
        specs.append((1, a, b))
        specs.append((2, a, b))
    for number, (kind, a, b) in enumerate(specs):
        across = term(kind, a, b, 0) + term(kind, a, b, 1) + term(kind, a, b, 2)
        total = window_lines(across)
        sums[number] = total[:, EDGE : EDGE + block]

    mask = mask_ref[...]
    scale = 3 * (2 * WIN_HALF + 1)

    def chunk_body(index, carry):
        start = pl.multiple_of(index * CHUNK, CHUNK)
        window = [sums[number, :, pl.ds(start, CHUNK)] / scale for number in range(len(specs))]
        powers = [window[a] + 1e-06 for a in range(dates)]
        coherence = {}
        for number, (a, b) in enumerate(pairs):
            factor = lax.rsqrt(powers[a] * powers[b])
            coherence[a, b] = (
                window[dates + 2 * number] * factor,
                window[dates + 2 * number + 1] * factor,
            )
        vector_real = [jnp.ones_like(powers[0]) for _ in range(dates)]
        vector_imag = [jnp.zeros_like(powers[0]) for _ in range(dates)]
        for iteration in range(POWER_ITERS):
            new_real = []
            new_imag = []
            for target in range(dates):
                acc_real = vector_real[target]
                acc_imag = vector_imag[target]
                for source in range(dates):
                    if source != target:
                        if target < source:
                            part_real, part_imag = coherence[target, source]
                        else:
                            part_real, part_imag = coherence[source, target]
                            part_imag = -part_imag
                        acc_real = (
                            acc_real + part_real * vector_real[source] - part_imag * vector_imag[source]
                        )
                        acc_imag = (
                            acc_imag + part_real * vector_imag[source] + part_imag * vector_real[source]
                        )
                new_real.append(acc_real)
                new_imag.append(acc_imag)
            mean_square = (
                sum(new_real[t] * new_real[t] + new_imag[t] * new_imag[t] for t in range(dates)) / dates
            )
            factor = lax.rsqrt(jnp.maximum(mean_square, 1.0))
            vector_real = [entry * factor for entry in new_real]
            vector_imag = [entry * factor for entry in new_imag]
        magnitude = sum(
            jnp.sqrt(coherence[pair][0] * coherence[pair][0] + coherence[pair][1] * coherence[pair][1])
            for pair in pairs
        ) / len(pairs)
        quality = mask * (0.05 + magnitude)
        vectors = vector_real + vector_imag
        for passes in range(SMOOTH_PASSES):
            denominator = quality + pltpu.roll(quality, 1, 0) + pltpu.roll(quality, rows - 1, 0)
            denominator = jnp.where(denominator > 0, denominator, 1.0)
            smoothed = []
            for entry in vectors:
                weighted = entry * quality
                numerator = weighted + pltpu.roll(weighted, 1, 0) + pltpu.roll(weighted, rows - 1, 0)
                smoothed.append(numerator / denominator)
            vectors = smoothed
        keep = slice(SMOOTH_PASSES, rows - SMOOTH_PASSES)
        for number, entry in enumerate(vectors):
            vec_ref[number // dates, number % dates, :, pl.ds(start, CHUNK)] = entry[keep]
        qual_ref[:, pl.ds(start, CHUNK)] = quality[keep]
        return carry

    lax.fori_loop(0, block // CHUNK, chunk_body, 0)


def link_and_smooth(extended, valid_mask):
    parts, dates, columns, lines = extended.shape
    rows = columns - 2
    kept = rows - 2 * SMOOTH_PASSES
    steps = lines // BLOCK
    per_block = BLOCK // EDGE
    edges = lines // EDGE
    mask = jnp.broadcast_to(valid_mask[:, None], (rows, CHUNK))
    return pl.pallas_call(
        link_kernel,
        grid=(steps,),
        in_specs=[
            pl.BlockSpec((rows, CHUNK), lambda i: (0, 0)),
            pl.BlockSpec((parts, dates, columns, EDGE), lambda i: (0, 0, 0, jnp.maximum(i * per_block - 1, 0))),
            pl.BlockSpec((parts, dates, columns, BLOCK), lambda i: (0, 0, 0, i)),
            pl.BlockSpec((parts, dates, columns, EDGE), lambda i: (0, 0, 0, jnp.minimum((i + 1) * per_block, edges - 1))),
        ],
        out_specs=[
            pl.BlockSpec((parts, dates, kept, BLOCK), lambda i: (0, 0, 0, i)),
            pl.BlockSpec((kept, BLOCK), lambda i: (0, i)),
        ],
        out_shape=[
            jax.ShapeDtypeStruct((parts, dates, kept, lines), jnp.float32),
            jax.ShapeDtypeStruct((kept, lines), jnp.float32),
        ],
        scratch_shapes=[
            pltpu.VMEM((parts, dates, columns, BLOCK + 2 * EDGE), jnp.float32),
            pltpu.VMEM((dates + dates * (dates - 1), rows, BLOCK), jnp.float32),
        ],
    )(mask, extended, extended, extended)


def split_up(x, dim, count):
    shape = x.shape
    tiles = x.reshape(*shape[:dim], count, shape[dim] // count, *shape[dim + 1 :])
    return jnp.moveaxis(tiles, dim, 0)


def laid_out(tiles, dim):
    shape = list(tiles.shape[1:])
    shape[dim] *= tiles.shape[0]
    return jnp.moveaxis(tiles, 0, dim).reshape(shape)


def one_exchange(x, axis, axes, splits, concats):
    sizes = [lax.axis_size(a) for a in axes]
    tiles = split_up(x, splits[0], sizes[0])
    tiles = jnp.moveaxis(split_up(tiles, splits[1] + 1, sizes[1]), 0, 1)
    inside = tiles.shape[2:]
    tiles = tiles.reshape(-1, *inside)
    tiles = lax.all_to_all(tiles, axis, split_axis=0, concat_axis=0, tiled=True)
    tiles = laid_out(tiles.reshape(*sizes, *inside), concats[0] + 1)
    return laid_out(tiles, concats[1])


def extended_2(x, sides, width):
    edges = {}
    for axis, dim in sides:
        count, length = (lax.axis_size(axis), x.shape[dim])
        up = [(i, (i + 1) % count) for i in range(count - 1)]
        last = lax.slice_in_dim(x, length - width, length, axis=dim)
        first = lax.slice_in_dim(x, 0, width, axis=dim)
        edges[dim] = (
            lax.ppermute(last, axis, up),
            lax.ppermute(first, axis, [(b, a) for a, b in up]),
        )
    done = []
    for _, dim in sides:
        low, high = edges[dim]
        around = [(width, width) if d in done else (0, 0) for d in range(x.ndim)]
        x = jnp.concatenate([jnp.pad(low, around), x, jnp.pad(high, around)], axis=dim)
        done.append(dim)
    return x


def dft_table(length, direction):
    counter = jnp.arange(length, dtype=jnp.int32)
    product = counter[:, None] * counter[None, :] % length
    angles = product.astype(jnp.float32) * (direction * 2.0 * math.pi / length)
    cosine = jnp.cos(angles)
    sine_part = jnp.sin(angles)
    return jnp.stack([jnp.stack([cosine, -sine_part]), jnp.stack([sine_part, cosine])])


def twiddle(outer_size, inner_size, direction):
    product = (
        jnp.arange(outer_size, dtype=jnp.int32)[:, None]
        * jnp.arange(inner_size, dtype=jnp.int32)[None, :]
        % (outer_size * inner_size)
    )
    angles = product.astype(jnp.float32) * (direction * 2.0 * math.pi / (outer_size * inner_size))
    return (jnp.cos(angles), jnp.sin(angles))


def rotate(values, cosine, sine_part):
    return jnp.stack(
        [values[0] * cosine - values[1] * sine_part, values[0] * sine_part + values[1] * cosine]
    )


def spectral_core(values, phases):
    outer_size = values.shape[-2]
    inner_size = values.shape[-1]
    values = jnp.einsum("pqkn,q...nm->p...km", dft_table(outer_size, -1), values, precision=HIGHEST)
    cos_part, sin_part = twiddle(outer_size, inner_size, -1)
    values = rotate(values, cos_part, sin_part)
    values = jnp.einsum("pqjm,q...km->p...kj", dft_table(inner_size, -1), values, precision=HIGHEST)
    phase_grid = phases.reshape(inner_size, outer_size).T
    values = rotate(values, jnp.cos(phase_grid), jnp.sin(phase_grid))
    values = jnp.einsum("pqmj,q...kj->p...km", dft_table(inner_size, 1), values, precision=HIGHEST)
    cos_part, sin_part = twiddle(outer_size, inner_size, 1)
    return rotate(values, cos_part, sin_part)


def azimuth_compress(values, phases):
    length = values.shape[-1]
    inner_size = 128
    outer_size = length // inner_size
    spectrum = spectral_core(values.reshape(values.shape[:-1] + (outer_size, inner_size)), phases)
    result = (
        jnp.einsum("pqnk,q...km->p...nm", dft_table(outer_size, 1), spectrum, precision=HIGHEST)
        / length
    )
    return result.reshape(values.shape)


def range_compress(values, phases, row_count):
    length = values.shape[-1]
    inner_size = 128
    outer_size = length // inner_size
    spectrum = spectral_core(values.reshape(values.shape[:-1] + (outer_size, inner_size)), phases)
    inverse_rows = dft_table(outer_size, 1)
    result = jnp.einsum("pqnk,qdlkm->pdnml", inverse_rows, spectrum, precision=HIGHEST) / length
    return result.reshape(2, values.shape[1], row_count * inner_size, values.shape[2])


def running_window(values):
    width = 2 * WIN_HALF + 1
    count = values.shape[-1]
    level = jnp.pad(values, ((0, 0), (0, 0), (WIN_HALF, WIN_HALF)))
    total = jnp.zeros_like(values)
    offset = 0
    span = 1
    while span <= width:
        if width & span:
            total = total + level[..., offset : offset + count]
            offset = offset + span
        level = level[..., :-span] + level[..., span:]
        span = span * 2
    return total


def link_block(real_ext, imag_ext, valid_mask):
    date_count = real_ext.shape[0]
    pair_list = [
        (former, latter) for former in range(date_count) for latter in range(former + 1, date_count)
    ]
    terms = [
        real_ext[former] * real_ext[former] + imag_ext[former] * imag_ext[former]
        for former in range(date_count)
    ]
    for former, latter in pair_list:
        terms.append(real_ext[former] * real_ext[latter] + imag_ext[former] * imag_ext[latter])
        terms.append(imag_ext[former] * real_ext[latter] - real_ext[former] * imag_ext[latter])
    stacked = jnp.stack(terms)
    across = stacked[:, :-2] + stacked[:, 1:-1] + stacked[:, 2:]
    window = running_window(across)
    window = window / (3 * (2 * WIN_HALF + 1))
    powers = window[:date_count] + 1e-06
    coherence = {}
    for number, pair in enumerate(pair_list):
        factor = lax.rsqrt(powers[pair[0]] * powers[pair[1]])
        coherence[pair] = (
            window[date_count + 2 * number] * factor,
            window[date_count + 2 * number + 1] * factor,
        )
    vector_real = [jnp.ones_like(powers[0]) for former in range(date_count)]
    vector_imag = [jnp.zeros_like(powers[0]) for former in range(date_count)]
    for iteration in range(POWER_ITERS):
        new_real = []
        new_imag = []
        for target in range(date_count):
            acc_real = vector_real[target]
            acc_imag = vector_imag[target]
            for source in range(date_count):
                if source != target:
                    if target < source:
                        part_real, part_imag = coherence[target, source]
                    else:
                        part_real, part_imag = coherence[source, target]
                        part_imag = -part_imag
                    acc_real = (
                        acc_real + part_real * vector_real[source] - part_imag * vector_imag[source]
                    )
                    acc_imag = (
                        acc_imag + part_real * vector_imag[source] + part_imag * vector_real[source]
                    )
            new_real.append(acc_real)
            new_imag.append(acc_imag)
        mean_square = (
            sum(
                (
                    new_real[target] * new_real[target] + new_imag[target] * new_imag[target]
                    for target in range(date_count)
                )
            )
            / date_count
        )
        factor = lax.rsqrt(jnp.maximum(mean_square, 1.0))
        vector_real = [entry * factor for entry in new_real]
        vector_imag = [entry * factor for entry in new_imag]
    magnitude = sum(
        (
            jnp.sqrt(
                coherence[pair][0] * coherence[pair][0] + coherence[pair][1] * coherence[pair][1]
            )
            for pair in pair_list
        )
    ) / len(pair_list)
    quality = valid_mask[:, None] * (0.05 + magnitude)
    vector = jnp.stack([jnp.stack(vector_real), jnp.stack(vector_imag)])
    return (vector, quality)


def shards(raw_echoes, range_phase, azimuth_phase, calibration):
    groups = lax.axis_size("date")
    group_dates = raw_echoes.shape[1]
    local_lines = raw_echoes.shape[2]
    length = raw_echoes.shape[3]
    outer_size = length // 128
    ranged = range_compress(raw_echoes.astype(jnp.float32), range_phase, outer_size)
    ranged = ranged.reshape(2, group_dates, groups, length // groups, local_lines)
    turned = one_exchange(ranged, ("date", "strip"), ("date", "strip"), (2, 3), (1, 4))
    focused = azimuth_compress(turned, azimuth_phase)
    all_dates = group_dates * groups
    column_count = calibration.shape[1]
    line_count = focused.shape[-1]
    image = focused.reshape(2, all_dates, column_count, line_count) * calibration[None, :, :, None]
    halo = 1 + SMOOTH_PASSES
    extended = extended_2(image, ((("date", "strip"), 2),), halo)
    total_columns = column_count * lax.axis_size("date") * lax.axis_size("strip")
    first = lax.axis_index(("date", "strip")) * column_count - SMOOTH_PASSES
    columns = first + jnp.arange(column_count + 2 * SMOOTH_PASSES, dtype=jnp.int32)
    valid_mask = ((columns >= 0) & (columns < total_columns)).astype(jnp.float32)
    vector, quality = link_and_smooth(extended, valid_mask)
    return (vector, quality)


def solution(mesh):
    in_specs = (P(None, "date", "strip", None), P(), P(), P(None, ("date", "strip")))
    out_specs = (P(None, None, ("date", "strip"), None), P(("date", "strip"), None))
    return jax.shard_map(shards, mesh=mesh, in_specs=in_specs, out_specs=out_specs, check_vma=False)
```

```python
import math

import jax
import jax.numpy as jnp
from jax import lax
from jax.experimental import pallas as pl
from jax.experimental.pallas import tpu as pltpu
from jax.sharding import PartitionSpec as P

WIN_HALF = 11
POWER_ITERS = 6
SMOOTH_PASSES = 2


HIGHEST = lax.Precision.HIGHEST
BLOCK = 1024
EDGE = 128
CHUNK = 128
ROWS = 8


def link_kernel(mask_ref, band_ref, prev_ref, cur_ref, next_ref, vec_ref, qual_ref, image, terms, high, low, sums):
    step = pl.program_id(0)
    last = pl.num_programs(0) - 1
    dates = cur_ref.shape[1]
    block = cur_ref.shape[3]
    padded = cur_ref.shape[2]
    image[:, :, :, EDGE : EDGE + block] = cur_ref[...]
    image[:, :, :, :EDGE] = jnp.where(step > 0, prev_ref[...], 0.0)
    image[:, :, :, EDGE + block :] = jnp.where(step < last, next_ref[...], 0.0)
    pairs = [(a, b) for a in range(dates) for b in range(a + 1, dates)]
    specs = [(0, a, a) for a in range(dates)]
    for a, b in pairs:
        specs.append((1, a, b))
        specs.append((2, a, b))

    for number, (kind, a, b) in enumerate(specs):
        ra, ia = image[0, a], image[1, a]
        if kind == 0:
            value = ra * ra + ia * ia
        else:
            rb, ib = image[0, b], image[1, b]
            if kind == 1:
                value = ra * rb + ia * ib
            else:
                value = ia * rb - ra * ib
        across = value + pltpu.roll(value, padded - 1, 0) + pltpu.roll(value, padded - 2, 0)
        terms[number * ROWS : (number + 1) * ROWS, :] = across[:ROWS]
    full = terms[...]
    top = full.astype(jnp.bfloat16)
    high[...] = top
    low[...] = (full - top.astype(jnp.float32)).astype(jnp.bfloat16)
    band = band_ref[...]
    for index in range(block // CHUNK):
        left = index * CHUNK
        window = jnp.dot(high[:, left : left + CHUNK + 2 * EDGE], band, preferred_element_type=jnp.float32)
        window = window + jnp.dot(low[:, left : left + CHUNK + 2 * EDGE], band, preferred_element_type=jnp.float32)
        sums[:, left : left + CHUNK] = window

    mask = mask_ref[...]
    inverse_scale = 1.0 / (3 * (2 * WIN_HALF + 1))

    def chunk_body(index, carry):
        start = pl.multiple_of(index * CHUNK, CHUNK)
        window = [
            sums[number * ROWS : (number + 1) * ROWS, pl.ds(start, CHUNK)] * inverse_scale
            for number in range(len(specs))
        ]
        powers = [window[a] + 1e-06 for a in range(dates)]
        coherence = {}
        for number, (a, b) in enumerate(pairs):
            factor = lax.rsqrt(powers[a] * powers[b])
            coherence[a, b] = (
                window[dates + 2 * number] * factor,
                window[dates + 2 * number + 1] * factor,
            )

        def entry(target, source):
            if target < source:
                return coherence[target, source]
            part_real, part_imag = coherence[source, target]
            return part_real, -part_imag

        new_real = []
        new_imag = []
        for target in range(dates):
            sources = [entry(target, source) for source in range(dates) if source != target]
            new_real.append(1.0 + sum(part[0] for part in sources))
            new_imag.append(sum(part[1] for part in sources))
        for iteration in range(POWER_ITERS):
            if iteration > 0:
                new_real = []
                new_imag = []
                for target in range(dates):
                    acc_real = vector_real[target]
                    acc_imag = vector_imag[target]
                    for source in range(dates):
                        if source != target:
                            part_real, part_imag = entry(target, source)
                            acc_real = (
                                acc_real + part_real * vector_real[source] - part_imag * vector_imag[source]
                            )
                            acc_imag = (
                                acc_imag + part_real * vector_imag[source] + part_imag * vector_real[source]
                            )
                    new_real.append(acc_real)
                    new_imag.append(acc_imag)
            mean_square = (
                sum(new_real[t] * new_real[t] + new_imag[t] * new_imag[t] for t in range(dates)) / dates
            )
            factor = lax.rsqrt(jnp.maximum(mean_square, 1.0))
            vector_real = [value * factor for value in new_real]
            vector_imag = [value * factor for value in new_imag]
        magnitude = sum(
            jnp.sqrt(coherence[pair][0] * coherence[pair][0] + coherence[pair][1] * coherence[pair][1])
            for pair in pairs
        ) / len(pairs)
        quality = mask * (0.05 + magnitude)
        vectors = vector_real + vector_imag
        for passes in range(SMOOTH_PASSES):
            denominator = quality + pltpu.roll(quality, 1, 0) + pltpu.roll(quality, ROWS - 1, 0)
            inverse = 1.0 / jnp.where(denominator > 0, denominator, 1.0)
            smoothed = []
            for value in vectors:
                weighted = value * quality
                numerator = weighted + pltpu.roll(weighted, 1, 0) + pltpu.roll(weighted, ROWS - 1, 0)
                smoothed.append(numerator * inverse)
            vectors = smoothed
        keep = slice(SMOOTH_PASSES, ROWS - SMOOTH_PASSES)
        for number, value in enumerate(vectors):
            vec_ref[number // dates, number % dates, :, pl.ds(start, CHUNK)] = value[keep]
        qual_ref[:, pl.ds(start, CHUNK)] = quality[keep]
        return carry

    lax.fori_loop(0, block // CHUNK, chunk_body, 0)


def link_and_smooth(extended, valid_mask):
    parts, dates, columns, lines = extended.shape
    padded = 16
    extended = jnp.concatenate(
        [extended, jnp.zeros((parts, dates, padded - columns, lines), extended.dtype)], axis=2
    )
    kept = ROWS - 2 * SMOOTH_PASSES
    steps = lines // BLOCK
    per_block = BLOCK // EDGE
    edges = lines // EDGE
    term_count = dates + dates * (dates - 1)
    mask = jnp.broadcast_to(valid_mask[:, None], (ROWS, CHUNK))
    offset = jnp.arange(CHUNK + 2 * EDGE, dtype=jnp.int32)[:, None] - EDGE - jnp.arange(CHUNK, dtype=jnp.int32)[None, :]
    band = (jnp.abs(offset) <= WIN_HALF).astype(jnp.bfloat16)
    width = BLOCK + 2 * EDGE
    return pl.pallas_call(
        link_kernel,
        grid=(steps,),
        in_specs=[
            pl.BlockSpec((ROWS, CHUNK), lambda i: (0, 0)),
            pl.BlockSpec((CHUNK + 2 * EDGE, CHUNK), lambda i: (0, 0)),
            pl.BlockSpec((parts, dates, padded, EDGE), lambda i: (0, 0, 0, jnp.maximum(i * per_block - 1, 0))),
            pl.BlockSpec((parts, dates, padded, BLOCK), lambda i: (0, 0, 0, i)),
            pl.BlockSpec((parts, dates, padded, EDGE), lambda i: (0, 0, 0, jnp.minimum((i + 1) * per_block, edges - 1))),
        ],
        out_specs=[
            pl.BlockSpec((parts, dates, kept, BLOCK), lambda i: (0, 0, 0, i)),
            pl.BlockSpec((kept, BLOCK), lambda i: (0, i)),
        ],
        out_shape=[
            jax.ShapeDtypeStruct((parts, dates, kept, lines), jnp.float32),
            jax.ShapeDtypeStruct((kept, lines), jnp.float32),
        ],
        scratch_shapes=[
            pltpu.VMEM((parts, dates, padded, width), jnp.float32),
            pltpu.VMEM((term_count * ROWS, width), jnp.float32),
            pltpu.VMEM((term_count * ROWS, width), jnp.bfloat16),
            pltpu.VMEM((term_count * ROWS, width), jnp.bfloat16),
            pltpu.VMEM((term_count * ROWS, BLOCK), jnp.float32),
        ],
    )(mask, band, extended, extended, extended)


def split_up(x, dim, count):
    shape = x.shape
    tiles = x.reshape(*shape[:dim], count, shape[dim] // count, *shape[dim + 1 :])
    return jnp.moveaxis(tiles, dim, 0)


def laid_out(tiles, dim):
    shape = list(tiles.shape[1:])
    shape[dim] *= tiles.shape[0]
    return jnp.moveaxis(tiles, 0, dim).reshape(shape)


def one_exchange(x, axis, axes, splits, concats):
    sizes = [lax.axis_size(a) for a in axes]
    tiles = split_up(x, splits[0], sizes[0])
    tiles = jnp.moveaxis(split_up(tiles, splits[1] + 1, sizes[1]), 0, 1)
    inside = tiles.shape[2:]
    tiles = tiles.reshape(-1, *inside)
    tiles = lax.all_to_all(tiles, axis, split_axis=0, concat_axis=0, tiled=True)
    tiles = laid_out(tiles.reshape(*sizes, *inside), concats[0] + 1)
    return laid_out(tiles, concats[1])


def extended_2(x, sides, width):
    edges = {}
    for axis, dim in sides:
        count, length = (lax.axis_size(axis), x.shape[dim])
        up = [(i, (i + 1) % count) for i in range(count - 1)]
        last = lax.slice_in_dim(x, length - width, length, axis=dim)
        first = lax.slice_in_dim(x, 0, width, axis=dim)
        edges[dim] = (
            lax.ppermute(last, axis, up),
            lax.ppermute(first, axis, [(b, a) for a, b in up]),
        )
    done = []
    for _, dim in sides:
        low, high = edges[dim]
        around = [(width, width) if d in done else (0, 0) for d in range(x.ndim)]
        x = jnp.concatenate([jnp.pad(low, around), x, jnp.pad(high, around)], axis=dim)
        done.append(dim)
    return x


def dft_table(length, direction):
    counter = jnp.arange(length, dtype=jnp.int32)
    product = counter[:, None] * counter[None, :] % length
    angles = product.astype(jnp.float32) * (direction * 2.0 * math.pi / length)
    cosine = jnp.cos(angles)
    sine_part = jnp.sin(angles)
    return jnp.stack([jnp.stack([cosine, -sine_part]), jnp.stack([sine_part, cosine])])


def twiddle(outer_size, inner_size, direction):
    product = (
        jnp.arange(outer_size, dtype=jnp.int32)[:, None]
        * jnp.arange(inner_size, dtype=jnp.int32)[None, :]
        % (outer_size * inner_size)
    )
    angles = product.astype(jnp.float32) * (direction * 2.0 * math.pi / (outer_size * inner_size))
    return (jnp.cos(angles), jnp.sin(angles))


def rotate(values, cosine, sine_part):
    return jnp.stack(
        [values[0] * cosine - values[1] * sine_part, values[0] * sine_part + values[1] * cosine]
    )


def spectral_core(values, phases):
    outer_size = values.shape[-2]
    inner_size = values.shape[-1]
    values = jnp.einsum("pqkn,q...nm->p...km", dft_table(outer_size, -1), values, precision=HIGHEST)
    cos_part, sin_part = twiddle(outer_size, inner_size, -1)
    values = rotate(values, cos_part, sin_part)
    values = jnp.einsum("pqjm,q...km->p...kj", dft_table(inner_size, -1), values, precision=HIGHEST)
    phase_grid = phases.reshape(inner_size, outer_size).T
    values = rotate(values, jnp.cos(phase_grid), jnp.sin(phase_grid))
    values = jnp.einsum("pqmj,q...kj->p...km", dft_table(inner_size, 1), values, precision=HIGHEST)
    cos_part, sin_part = twiddle(outer_size, inner_size, 1)
    return rotate(values, cos_part, sin_part)


def azimuth_compress(values, phases):
    length = values.shape[-1]
    inner_size = 128
    outer_size = length // inner_size
    spectrum = spectral_core(values.reshape(values.shape[:-1] + (outer_size, inner_size)), phases)
    result = (
        jnp.einsum("pqnk,q...km->p...nm", dft_table(outer_size, 1), spectrum, precision=HIGHEST)
        / length
    )
    return result.reshape(values.shape)


def range_compress(values, phases, row_count):
    length = values.shape[-1]
    inner_size = 128
    outer_size = length // inner_size
    spectrum = spectral_core(values.reshape(values.shape[:-1] + (outer_size, inner_size)), phases)
    inverse_rows = dft_table(outer_size, 1)
    result = jnp.einsum("pqnk,qdlkm->pdnml", inverse_rows, spectrum, precision=HIGHEST) / length
    return result.reshape(2, values.shape[1], row_count * inner_size, values.shape[2])


def running_window(values):
    width = 2 * WIN_HALF + 1
    count = values.shape[-1]
    level = jnp.pad(values, ((0, 0), (0, 0), (WIN_HALF, WIN_HALF)))
    total = jnp.zeros_like(values)
    offset = 0
    span = 1
    while span <= width:
        if width & span:
            total = total + level[..., offset : offset + count]
            offset = offset + span
        level = level[..., :-span] + level[..., span:]
        span = span * 2
    return total


def link_block(real_ext, imag_ext, valid_mask):
    date_count = real_ext.shape[0]
    pair_list = [
        (former, latter) for former in range(date_count) for latter in range(former + 1, date_count)
    ]
    terms = [
        real_ext[former] * real_ext[former] + imag_ext[former] * imag_ext[former]
        for former in range(date_count)
    ]
    for former, latter in pair_list:
        terms.append(real_ext[former] * real_ext[latter] + imag_ext[former] * imag_ext[latter])
        terms.append(imag_ext[former] * real_ext[latter] - real_ext[former] * imag_ext[latter])
    stacked = jnp.stack(terms)
    across = stacked[:, :-2] + stacked[:, 1:-1] + stacked[:, 2:]
    window = running_window(across)
    window = window / (3 * (2 * WIN_HALF + 1))
    powers = window[:date_count] + 1e-06
    coherence = {}
    for number, pair in enumerate(pair_list):
        factor = lax.rsqrt(powers[pair[0]] * powers[pair[1]])
        coherence[pair] = (
            window[date_count + 2 * number] * factor,
            window[date_count + 2 * number + 1] * factor,
        )
    vector_real = [jnp.ones_like(powers[0]) for former in range(date_count)]
    vector_imag = [jnp.zeros_like(powers[0]) for former in range(date_count)]
    for iteration in range(POWER_ITERS):
        new_real = []
        new_imag = []
        for target in range(date_count):
            acc_real = vector_real[target]
            acc_imag = vector_imag[target]
            for source in range(date_count):
                if source != target:
                    if target < source:
                        part_real, part_imag = coherence[target, source]
                    else:
                        part_real, part_imag = coherence[source, target]
                        part_imag = -part_imag
                    acc_real = (
                        acc_real + part_real * vector_real[source] - part_imag * vector_imag[source]
                    )
                    acc_imag = (
                        acc_imag + part_real * vector_imag[source] + part_imag * vector_real[source]
                    )
            new_real.append(acc_real)
            new_imag.append(acc_imag)
        mean_square = (
            sum(
                (
                    new_real[target] * new_real[target] + new_imag[target] * new_imag[target]
                    for target in range(date_count)
                )
            )
            / date_count
        )
        factor = lax.rsqrt(jnp.maximum(mean_square, 1.0))
        vector_real = [entry * factor for entry in new_real]
        vector_imag = [entry * factor for entry in new_imag]
    magnitude = sum(
        (
            jnp.sqrt(
                coherence[pair][0] * coherence[pair][0] + coherence[pair][1] * coherence[pair][1]
            )
            for pair in pair_list
        )
    ) / len(pair_list)
    quality = valid_mask[:, None] * (0.05 + magnitude)
    vector = jnp.stack([jnp.stack(vector_real), jnp.stack(vector_imag)])
    return (vector, quality)


def shards(raw_echoes, range_phase, azimuth_phase, calibration):
    groups = lax.axis_size("date")
    group_dates = raw_echoes.shape[1]
    local_lines = raw_echoes.shape[2]
    length = raw_echoes.shape[3]
    outer_size = length // 128
    ranged = range_compress(raw_echoes.astype(jnp.float32), range_phase, outer_size)
    ranged = ranged.reshape(2, group_dates, groups, length // groups, local_lines)
    turned = one_exchange(ranged, ("date", "strip"), ("date", "strip"), (2, 3), (1, 4))
    focused = azimuth_compress(turned, azimuth_phase)
    all_dates = group_dates * groups
    column_count = calibration.shape[1]
    line_count = focused.shape[-1]
    image = focused.reshape(2, all_dates, column_count, line_count) * calibration[None, :, :, None]
    halo = 1 + SMOOTH_PASSES
    extended = extended_2(image, ((("date", "strip"), 2),), halo)
    total_columns = column_count * lax.axis_size("date") * lax.axis_size("strip")
    first = lax.axis_index(("date", "strip")) * column_count - SMOOTH_PASSES
    columns = first + jnp.arange(column_count + 2 * SMOOTH_PASSES, dtype=jnp.int32)
    valid_mask = ((columns >= 0) & (columns < total_columns)).astype(jnp.float32)
    vector, quality = link_and_smooth(extended, valid_mask)
    return (vector, quality)


def solution(mesh):
    in_specs = (P(None, "date", "strip", None), P(), P(), P(None, ("date", "strip")))
    out_specs = (P(None, None, ("date", "strip"), None), P(("date", "strip"), None))
    return jax.shard_map(shards, mesh=mesh, in_specs=in_specs, out_specs=out_specs, check_vma=False)
```

```python
import math

import jax
import jax.numpy as jnp
from jax import lax
from jax.experimental import pallas as pl
from jax.experimental.pallas import tpu as pltpu
from jax.sharding import PartitionSpec as P

WIN_HALF = 11
POWER_ITERS = 6
SMOOTH_PASSES = 2


HIGHEST = lax.Precision.HIGHEST
BLOCK = 1024
EDGE = 128
CHUNK = 128
ROWS = 8


def link_kernel(mask_ref, band_ref, *refs):
    pieces = refs[:9]
    vec_ref, qual_ref, image, terms, high, low, sums = refs[9:]
    step = pl.program_id(0)
    last = pl.num_programs(0) - 1
    dates = pieces[1].shape[1]
    block = pieces[1].shape[3]
    padded = image.shape[2]
    row = 0
    for number in range(3):
        prev_ref, cur_ref, next_ref = pieces[3 * number : 3 * number + 3]
        count = cur_ref.shape[2]
        rows = slice(row, row + count)
        image[:, :, rows, EDGE : EDGE + block] = cur_ref[...]
        image[:, :, rows, :EDGE] = jnp.where(step > 0, prev_ref[...], 0.0)
        image[:, :, rows, EDGE + block :] = jnp.where(step < last, next_ref[...], 0.0)
        row += count
    image[:, :, row:, :] = jnp.zeros((image.shape[0], dates, padded - row, image.shape[3]), jnp.float32)
    pairs = [(a, b) for a in range(dates) for b in range(a + 1, dates)]
    specs = [(0, a, a) for a in range(dates)]
    for a, b in pairs:
        specs.append((1, a, b))
        specs.append((2, a, b))

    for number, (kind, a, b) in enumerate(specs):
        ra, ia = image[0, a], image[1, a]
        if kind == 0:
            value = ra * ra + ia * ia
        else:
            rb, ib = image[0, b], image[1, b]
            if kind == 1:
                value = ra * rb + ia * ib
            else:
                value = ia * rb - ra * ib
        across = value + pltpu.roll(value, padded - 1, 0) + pltpu.roll(value, padded - 2, 0)
        terms[number * ROWS : (number + 1) * ROWS, :] = across[:ROWS]
    full = terms[...]
    top = full.astype(jnp.bfloat16)
    high[...] = top
    low[...] = (full - top.astype(jnp.float32)).astype(jnp.bfloat16)
    band = band_ref[...]
    for index in range(block // CHUNK):
        left = index * CHUNK
        window = jnp.dot(high[:, left : left + CHUNK + 2 * EDGE], band, preferred_element_type=jnp.float32)
        window = window + jnp.dot(low[:, left : left + CHUNK + 2 * EDGE], band, preferred_element_type=jnp.float32)
        sums[:, left : left + CHUNK] = window

    mask = mask_ref[...]
    inverse_scale = 1.0 / (3 * (2 * WIN_HALF + 1))

    def chunk_body(index, carry):
        start = pl.multiple_of(index * CHUNK, CHUNK)
        window = [
            sums[number * ROWS : (number + 1) * ROWS, pl.ds(start, CHUNK)] * inverse_scale
            for number in range(len(specs))
        ]
        powers = [window[a] + 1e-06 for a in range(dates)]
        coherence = {}
        for number, (a, b) in enumerate(pairs):
            factor = lax.rsqrt(powers[a] * powers[b])
            coherence[a, b] = (
                window[dates + 2 * number] * factor,
                window[dates + 2 * number + 1] * factor,
            )

        def entry(target, source):
            if target < source:
                return coherence[target, source]
            part_real, part_imag = coherence[source, target]
            return part_real, -part_imag

        new_real = []
        new_imag = []
        for target in range(dates):
            sources = [entry(target, source) for source in range(dates) if source != target]
            new_real.append(1.0 + sum(part[0] for part in sources))
            new_imag.append(sum(part[1] for part in sources))
        for iteration in range(POWER_ITERS):
            if iteration > 0:
                new_real = []
                new_imag = []
                for target in range(dates):
                    acc_real = vector_real[target]
                    acc_imag = vector_imag[target]
                    for source in range(dates):
                        if source != target:
                            part_real, part_imag = entry(target, source)
                            acc_real = (
                                acc_real + part_real * vector_real[source] - part_imag * vector_imag[source]
                            )
                            acc_imag = (
                                acc_imag + part_real * vector_imag[source] + part_imag * vector_real[source]
                            )
                    new_real.append(acc_real)
                    new_imag.append(acc_imag)
            mean_square = (
                sum(new_real[t] * new_real[t] + new_imag[t] * new_imag[t] for t in range(dates)) / dates
            )
            factor = lax.rsqrt(jnp.maximum(mean_square, 1.0))
            vector_real = [value * factor for value in new_real]
            vector_imag = [value * factor for value in new_imag]
        magnitude = sum(
            jnp.sqrt(coherence[pair][0] * coherence[pair][0] + coherence[pair][1] * coherence[pair][1])
            for pair in pairs
        ) / len(pairs)
        quality = mask * (0.05 + magnitude)
        vectors = vector_real + vector_imag
        for passes in range(SMOOTH_PASSES):
            denominator = quality + pltpu.roll(quality, 1, 0) + pltpu.roll(quality, ROWS - 1, 0)
            inverse = 1.0 / jnp.where(denominator > 0, denominator, 1.0)
            smoothed = []
            for value in vectors:
                weighted = value * quality
                numerator = weighted + pltpu.roll(weighted, 1, 0) + pltpu.roll(weighted, ROWS - 1, 0)
                smoothed.append(numerator * inverse)
            vectors = smoothed
        keep = slice(SMOOTH_PASSES, ROWS - SMOOTH_PASSES)
        for number, value in enumerate(vectors):
            vec_ref[number // dates, number % dates, :, pl.ds(start, CHUNK)] = value[keep]
        qual_ref[:, pl.ds(start, CHUNK)] = quality[keep]
        return carry

    lax.fori_loop(0, block // CHUNK, chunk_body, 0)


def link_and_smooth(pieces, valid_mask):
    parts, dates, _, lines = pieces[1].shape
    padded = 16
    kept = ROWS - 2 * SMOOTH_PASSES
    steps = lines // BLOCK
    per_block = BLOCK // EDGE
    edges = lines // EDGE
    term_count = dates + dates * (dates - 1)
    mask = jnp.broadcast_to(valid_mask[:, None], (ROWS, CHUNK))
    offset = jnp.arange(CHUNK + 2 * EDGE, dtype=jnp.int32)[:, None] - EDGE - jnp.arange(CHUNK, dtype=jnp.int32)[None, :]
    band = (jnp.abs(offset) <= WIN_HALF).astype(jnp.bfloat16)
    width = BLOCK + 2 * EDGE
    piece_specs = []
    operands = []
    for piece in pieces:
        count = piece.shape[2]
        piece_specs += [
            pl.BlockSpec((parts, dates, count, EDGE), lambda i: (0, 0, 0, jnp.maximum(i * per_block - 1, 0))),
            pl.BlockSpec((parts, dates, count, BLOCK), lambda i: (0, 0, 0, i)),
            pl.BlockSpec((parts, dates, count, EDGE), lambda i: (0, 0, 0, jnp.minimum((i + 1) * per_block, edges - 1))),
        ]
        operands += [piece, piece, piece]
    return pl.pallas_call(
        link_kernel,
        grid=(steps,),
        in_specs=[
            pl.BlockSpec((ROWS, CHUNK), lambda i: (0, 0)),
            pl.BlockSpec((CHUNK + 2 * EDGE, CHUNK), lambda i: (0, 0)),
        ]
        + piece_specs,
        out_specs=[
            pl.BlockSpec((parts, dates, kept, BLOCK), lambda i: (0, 0, 0, i)),
            pl.BlockSpec((kept, BLOCK), lambda i: (0, i)),
        ],
        out_shape=[
            jax.ShapeDtypeStruct((parts, dates, kept, lines), jnp.float32),
            jax.ShapeDtypeStruct((kept, lines), jnp.float32),
        ],
        scratch_shapes=[
            pltpu.VMEM((parts, dates, padded, width), jnp.float32),
            pltpu.VMEM((term_count * ROWS, width), jnp.float32),
            pltpu.VMEM((term_count * ROWS, width), jnp.bfloat16),
            pltpu.VMEM((term_count * ROWS, width), jnp.bfloat16),
            pltpu.VMEM((term_count * ROWS, BLOCK), jnp.float32),
        ],
    )(mask, band, *operands)


def split_up(x, dim, count):
    shape = x.shape
    tiles = x.reshape(*shape[:dim], count, shape[dim] // count, *shape[dim + 1 :])
    return jnp.moveaxis(tiles, dim, 0)


def laid_out(tiles, dim):
    shape = list(tiles.shape[1:])
    shape[dim] *= tiles.shape[0]
    return jnp.moveaxis(tiles, 0, dim).reshape(shape)


def one_exchange(x, axis, axes, splits, concats):
    sizes = [lax.axis_size(a) for a in axes]
    tiles = split_up(x, splits[0], sizes[0])
    tiles = jnp.moveaxis(split_up(tiles, splits[1] + 1, sizes[1]), 0, 1)
    inside = tiles.shape[2:]
    tiles = tiles.reshape(-1, *inside)
    tiles = lax.all_to_all(tiles, axis, split_axis=0, concat_axis=0, tiled=True)
    tiles = laid_out(tiles.reshape(*sizes, *inside), concats[0] + 1)
    return laid_out(tiles, concats[1])


def extended_2(x, sides, width):
    edges = {}
    for axis, dim in sides:
        count, length = (lax.axis_size(axis), x.shape[dim])
        up = [(i, (i + 1) % count) for i in range(count - 1)]
        last = lax.slice_in_dim(x, length - width, length, axis=dim)
        first = lax.slice_in_dim(x, 0, width, axis=dim)
        edges[dim] = (
            lax.ppermute(last, axis, up),
            lax.ppermute(first, axis, [(b, a) for a, b in up]),
        )
    done = []
    for _, dim in sides:
        low, high = edges[dim]
        around = [(width, width) if d in done else (0, 0) for d in range(x.ndim)]
        x = jnp.concatenate([jnp.pad(low, around), x, jnp.pad(high, around)], axis=dim)
        done.append(dim)
    return x


def dft_table(length, direction):
    counter = jnp.arange(length, dtype=jnp.int32)
    product = counter[:, None] * counter[None, :] % length
    angles = product.astype(jnp.float32) * (direction * 2.0 * math.pi / length)
    cosine = jnp.cos(angles)
    sine_part = jnp.sin(angles)
    return jnp.stack([jnp.stack([cosine, -sine_part]), jnp.stack([sine_part, cosine])])


def twiddle(outer_size, inner_size, direction):
    product = (
        jnp.arange(outer_size, dtype=jnp.int32)[:, None]
        * jnp.arange(inner_size, dtype=jnp.int32)[None, :]
        % (outer_size * inner_size)
    )
    angles = product.astype(jnp.float32) * (direction * 2.0 * math.pi / (outer_size * inner_size))
    return (jnp.cos(angles), jnp.sin(angles))


def rotate(values, cosine, sine_part):
    return jnp.stack(
        [values[0] * cosine - values[1] * sine_part, values[0] * sine_part + values[1] * cosine]
    )


def spectral_core(values, phases):
    outer_size = values.shape[-2]
    inner_size = values.shape[-1]
    values = jnp.einsum("pqkn,q...nm->p...km", dft_table(outer_size, -1), values, precision=HIGHEST)
    cos_part, sin_part = twiddle(outer_size, inner_size, -1)
    values = rotate(values, cos_part, sin_part)
    values = jnp.einsum("pqjm,q...km->p...kj", dft_table(inner_size, -1), values, precision=HIGHEST)
    phase_grid = phases.reshape(inner_size, outer_size).T
    values = rotate(values, jnp.cos(phase_grid), jnp.sin(phase_grid))
    values = jnp.einsum("pqmj,q...kj->p...km", dft_table(inner_size, 1), values, precision=HIGHEST)
    cos_part, sin_part = twiddle(outer_size, inner_size, 1)
    return rotate(values, cos_part, sin_part)


def azimuth_compress(values, phases):
    length = values.shape[-1]
    inner_size = 128
    outer_size = length // inner_size
    spectrum = spectral_core(values.reshape(values.shape[:-1] + (outer_size, inner_size)), phases)
    result = (
        jnp.einsum("pqnk,q...km->p...nm", dft_table(outer_size, 1), spectrum, precision=HIGHEST)
        / length
    )
    return result.reshape(values.shape)


def range_compress(values, phases, row_count):
    length = values.shape[-1]
    inner_size = 128
    outer_size = length // inner_size
    spectrum = spectral_core(values.reshape(values.shape[:-1] + (outer_size, inner_size)), phases)
    inverse_rows = dft_table(outer_size, 1)
    result = jnp.einsum("pqnk,qdlkm->pdnml", inverse_rows, spectrum, precision=HIGHEST) / length
    return result.reshape(2, values.shape[1], row_count * inner_size, values.shape[2])


def range_blocks(values, phases):
    length = values.shape[-1]
    inner_size = 128
    outer_size = length // inner_size
    spectrum = spectral_core(values.reshape(values.shape[:-1] + (outer_size, inner_size)), phases)
    inverse_rows = dft_table(outer_size, 1)
    return jnp.einsum("pqnk,qdlkm->nmpdl", inverse_rows, spectrum, precision=HIGHEST) / length


def running_window(values):
    width = 2 * WIN_HALF + 1
    count = values.shape[-1]
    level = jnp.pad(values, ((0, 0), (0, 0), (WIN_HALF, WIN_HALF)))
    total = jnp.zeros_like(values)
    offset = 0
    span = 1
    while span <= width:
        if width & span:
            total = total + level[..., offset : offset + count]
            offset = offset + span
        level = level[..., :-span] + level[..., span:]
        span = span * 2
    return total


def link_block(real_ext, imag_ext, valid_mask):
    date_count = real_ext.shape[0]
    pair_list = [
        (former, latter) for former in range(date_count) for latter in range(former + 1, date_count)
    ]
    terms = [
        real_ext[former] * real_ext[former] + imag_ext[former] * imag_ext[former]
        for former in range(date_count)
    ]
    for former, latter in pair_list:
        terms.append(real_ext[former] * real_ext[latter] + imag_ext[former] * imag_ext[latter])
        terms.append(imag_ext[former] * real_ext[latter] - real_ext[former] * imag_ext[latter])
    stacked = jnp.stack(terms)
    across = stacked[:, :-2] + stacked[:, 1:-1] + stacked[:, 2:]
    window = running_window(across)
    window = window / (3 * (2 * WIN_HALF + 1))
    powers = window[:date_count] + 1e-06
    coherence = {}
    for number, pair in enumerate(pair_list):
        factor = lax.rsqrt(powers[pair[0]] * powers[pair[1]])
        coherence[pair] = (
            window[date_count + 2 * number] * factor,
            window[date_count + 2 * number + 1] * factor,
        )
    vector_real = [jnp.ones_like(powers[0]) for former in range(date_count)]
    vector_imag = [jnp.zeros_like(powers[0]) for former in range(date_count)]
    for iteration in range(POWER_ITERS):
        new_real = []
        new_imag = []
        for target in range(date_count):
            acc_real = vector_real[target]
            acc_imag = vector_imag[target]
            for source in range(date_count):
                if source != target:
                    if target < source:
                        part_real, part_imag = coherence[target, source]
                    else:
                        part_real, part_imag = coherence[source, target]
                        part_imag = -part_imag
                    acc_real = (
                        acc_real + part_real * vector_real[source] - part_imag * vector_imag[source]
                    )
                    acc_imag = (
                        acc_imag + part_real * vector_imag[source] + part_imag * vector_real[source]
                    )
            new_real.append(acc_real)
            new_imag.append(acc_imag)
        mean_square = (
            sum(
                (
                    new_real[target] * new_real[target] + new_imag[target] * new_imag[target]
                    for target in range(date_count)
                )
            )
            / date_count
        )
        factor = lax.rsqrt(jnp.maximum(mean_square, 1.0))
        vector_real = [entry * factor for entry in new_real]
        vector_imag = [entry * factor for entry in new_imag]
    magnitude = sum(
        (
            jnp.sqrt(
                coherence[pair][0] * coherence[pair][0] + coherence[pair][1] * coherence[pair][1]
            )
            for pair in pair_list
        )
    ) / len(pair_list)
    quality = valid_mask[:, None] * (0.05 + magnitude)
    vector = jnp.stack([jnp.stack(vector_real), jnp.stack(vector_imag)])
    return (vector, quality)


def shards(raw_echoes, range_phase, azimuth_phase, calibration):
    groups = lax.axis_size("date")
    group_dates = raw_echoes.shape[1]
    local_lines = raw_echoes.shape[2]
    length = raw_echoes.shape[3]
    outer_size = length // 128
    devices = groups * lax.axis_size("strip")
    ranged = range_blocks(raw_echoes.astype(jnp.float32), range_phase)
    tiles = ranged.reshape(devices, -1, 128)
    tiles = lax.all_to_all(tiles, ("date", "strip"), 0, 0, tiled=True)
    strips = devices // groups
    block_range = length // devices
    received = tiles.reshape(groups, strips, block_range, 2, group_dates, local_lines)
    turned = received.transpose(3, 0, 4, 2, 1, 5).reshape(
        2, groups * group_dates, block_range, strips * local_lines
    )
    focused = azimuth_compress(turned, azimuth_phase)
    all_dates = group_dates * groups
    column_count = calibration.shape[1]
    line_count = focused.shape[-1]
    image = focused.reshape(2, all_dates, column_count, line_count) * calibration[None, :, :, None]
    halo = 1 + SMOOTH_PASSES
    axes = ("date", "strip")
    count = lax.axis_size("date") * lax.axis_size("strip")
    up = [(i, i + 1) for i in range(count - 1)]
    low = lax.ppermute(image[:, :, column_count - halo :], axes, up)
    high = lax.ppermute(image[:, :, :halo], axes, [(b, a) for a, b in up])
    total_columns = column_count * lax.axis_size("date") * lax.axis_size("strip")
    first = lax.axis_index(("date", "strip")) * column_count - SMOOTH_PASSES
    columns = first + jnp.arange(column_count + 2 * SMOOTH_PASSES, dtype=jnp.int32)
    valid_mask = ((columns >= 0) & (columns < total_columns)).astype(jnp.float32)
    vector, quality = link_and_smooth((low, image, high), valid_mask)
    return (vector, quality)


def solution(mesh):
    in_specs = (P(None, "date", "strip", None), P(), P(), P(None, ("date", "strip")))
    out_specs = (P(None, None, ("date", "strip"), None), P(("date", "strip"), None))
    return jax.shard_map(shards, mesh=mesh, in_specs=in_specs, out_specs=out_specs, check_vma=False)
```

```python
import math

import numpy as np

import jax
import jax.numpy as jnp
from jax import lax
from jax.experimental import pallas as pl
from jax.experimental.pallas import tpu as pltpu
from jax.sharding import PartitionSpec as P

WIN_HALF = 11
POWER_ITERS = 6
SMOOTH_PASSES = 2


HIGHEST = lax.Precision.HIGHEST
BLOCK = 1024
EDGE = 128
CHUNK = 128
ROWS = 8


def link_kernel(mask_ref, band_ref, *refs):
    pieces = refs[:9]
    vec_ref, qual_ref, image, terms, high, low, sums = refs[9:]
    step = pl.program_id(0)
    last = pl.num_programs(0) - 1
    dates = pieces[4].shape[1]
    block = pieces[4].shape[3]
    padded = image.shape[2]
    row = 0
    for number in range(3):
        prev_ref, cur_ref, next_ref = pieces[3 * number : 3 * number + 3]
        if len(cur_ref.shape) == 4:
            count = cur_ref.shape[2]
            rows = slice(row, row + count)
            image[:, :, rows, EDGE : EDGE + block] = cur_ref[...]
            image[:, :, rows, :EDGE] = jnp.where(step > 0, prev_ref[...], 0.0)
            image[:, :, rows, EDGE + block :] = jnp.where(step < last, next_ref[...], 0.0)
        else:
            count = cur_ref.shape[0] // (image.shape[0] * dates)
            rows = slice(row, row + count)
            for p in range(image.shape[0]):
                for d in range(dates):
                    source = slice((p * dates + d) * count, (p * dates + d + 1) * count)
                    image[p, d, rows, EDGE : EDGE + block] = cur_ref[source, :]
                    image[p, d, rows, :EDGE] = jnp.where(step > 0, prev_ref[source, :], 0.0)
                    image[p, d, rows, EDGE + block :] = jnp.where(step < last, next_ref[source, :], 0.0)
        row += count
    image[:, :, row:, :] = jnp.zeros((image.shape[0], dates, padded - row, image.shape[3]), jnp.float32)
    pairs = [(a, b) for a in range(dates) for b in range(a + 1, dates)]
    specs = [(0, a, a) for a in range(dates)]
    for a, b in pairs:
        specs.append((1, a, b))
        specs.append((2, a, b))

    for number, (kind, a, b) in enumerate(specs):
        ra, ia = image[0, a], image[1, a]
        if kind == 0:
            value = ra * ra + ia * ia
        else:
            rb, ib = image[0, b], image[1, b]
            if kind == 1:
                value = ra * rb + ia * ib
            else:
                value = ia * rb - ra * ib
        across = value + pltpu.roll(value, padded - 1, 0) + pltpu.roll(value, padded - 2, 0)
        terms[number * ROWS : (number + 1) * ROWS, :] = across[:ROWS]
    full = terms[...]
    top = full.astype(jnp.bfloat16)
    high[...] = top
    low[...] = (full - top.astype(jnp.float32)).astype(jnp.bfloat16)
    band = band_ref[...]
    for index in range(block // CHUNK):
        left = index * CHUNK
        window = jnp.dot(high[:, left : left + CHUNK + 2 * EDGE], band, preferred_element_type=jnp.float32)
        window = window + jnp.dot(low[:, left : left + CHUNK + 2 * EDGE], band, preferred_element_type=jnp.float32)
        sums[:, left : left + CHUNK] = window

    mask = mask_ref[...]
    inverse_scale = 1.0 / (3 * (2 * WIN_HALF + 1))

    def chunk_body(index, carry):
        start = pl.multiple_of(index * CHUNK, CHUNK)
        window = [
            sums[number * ROWS : (number + 1) * ROWS, pl.ds(start, CHUNK)] * inverse_scale
            for number in range(len(specs))
        ]
        powers = [window[a] + 1e-06 for a in range(dates)]
        coherence = {}
        for number, (a, b) in enumerate(pairs):
            factor = lax.rsqrt(powers[a] * powers[b])
            coherence[a, b] = (
                window[dates + 2 * number] * factor,
                window[dates + 2 * number + 1] * factor,
            )

        def entry(target, source):
            if target < source:
                return coherence[target, source]
            part_real, part_imag = coherence[source, target]
            return part_real, -part_imag

        new_real = []
        new_imag = []
        for target in range(dates):
            sources = [entry(target, source) for source in range(dates) if source != target]
            new_real.append(1.0 + sum(part[0] for part in sources))
            new_imag.append(sum(part[1] for part in sources))
        for iteration in range(POWER_ITERS):
            if iteration > 0:
                new_real = []
                new_imag = []
                for target in range(dates):
                    acc_real = vector_real[target]
                    acc_imag = vector_imag[target]
                    for source in range(dates):
                        if source != target:
                            part_real, part_imag = entry(target, source)
                            acc_real = (
                                acc_real + part_real * vector_real[source] - part_imag * vector_imag[source]
                            )
                            acc_imag = (
                                acc_imag + part_real * vector_imag[source] + part_imag * vector_real[source]
                            )
                    new_real.append(acc_real)
                    new_imag.append(acc_imag)
            mean_square = (
                sum(new_real[t] * new_real[t] + new_imag[t] * new_imag[t] for t in range(dates)) / dates
            )
            factor = lax.rsqrt(jnp.maximum(mean_square, 1.0))
            vector_real = [value * factor for value in new_real]
            vector_imag = [value * factor for value in new_imag]
        magnitude = sum(
            jnp.sqrt(coherence[pair][0] * coherence[pair][0] + coherence[pair][1] * coherence[pair][1])
            for pair in pairs
        ) / len(pairs)
        quality = mask * (0.05 + magnitude)
        vectors = vector_real + vector_imag
        for passes in range(SMOOTH_PASSES):
            denominator = quality + pltpu.roll(quality, 1, 0) + pltpu.roll(quality, ROWS - 1, 0)
            inverse = 1.0 / jnp.where(denominator > 0, denominator, 1.0)
            smoothed = []
            for value in vectors:
                weighted = value * quality
                numerator = weighted + pltpu.roll(weighted, 1, 0) + pltpu.roll(weighted, ROWS - 1, 0)
                smoothed.append(numerator * inverse)
            vectors = smoothed
        keep = slice(SMOOTH_PASSES, ROWS - SMOOTH_PASSES)
        for number, value in enumerate(vectors):
            vec_ref[number // dates, number % dates, :, pl.ds(start, CHUNK)] = value[keep]
        qual_ref[:, pl.ds(start, CHUNK)] = quality[keep]
        return carry

    lax.fori_loop(0, block // CHUNK, chunk_body, 0)


def link_and_smooth(pieces, valid_mask):
    parts, dates, _, lines = pieces[1].shape
    assert all(piece.shape[-1] == lines for piece in pieces)
    padded = 16
    kept = ROWS - 2 * SMOOTH_PASSES
    steps = lines // BLOCK
    per_block = BLOCK // EDGE
    edges = lines // EDGE
    term_count = dates + dates * (dates - 1)
    mask = jnp.broadcast_to(valid_mask[:, None], (ROWS, CHUNK))
    offset = np.arange(CHUNK + 2 * EDGE)[:, None] - EDGE - np.arange(CHUNK)[None, :]
    band = jnp.asarray(np.abs(offset) <= WIN_HALF, jnp.bfloat16)
    width = BLOCK + 2 * EDGE
    piece_specs = []
    operands = []
    for piece in pieces:
        lead = (0,) * (piece.ndim - 1)
        piece_specs += [
            pl.BlockSpec(piece.shape[:-1] + (EDGE,), lambda i, lead=lead: lead + (jnp.maximum(i * per_block - 1, 0),)),
            pl.BlockSpec(piece.shape[:-1] + (BLOCK,), lambda i, lead=lead: lead + (i,)),
            pl.BlockSpec(piece.shape[:-1] + (EDGE,), lambda i, lead=lead: lead + (jnp.minimum((i + 1) * per_block, edges - 1),)),
        ]
        operands += [piece, piece, piece]
    return pl.pallas_call(
        link_kernel,
        grid=(steps,),
        in_specs=[
            pl.BlockSpec((ROWS, CHUNK), lambda i: (0, 0)),
            pl.BlockSpec((CHUNK + 2 * EDGE, CHUNK), lambda i: (0, 0)),
        ]
        + piece_specs,
        out_specs=[
            pl.BlockSpec((parts, dates, kept, BLOCK), lambda i: (0, 0, 0, i)),
            pl.BlockSpec((kept, BLOCK), lambda i: (0, i)),
        ],
        out_shape=[
            jax.ShapeDtypeStruct((parts, dates, kept, lines), jnp.float32),
            jax.ShapeDtypeStruct((kept, lines), jnp.float32),
        ],
        scratch_shapes=[
            pltpu.VMEM((parts, dates, padded, width), jnp.float32),
            pltpu.VMEM((term_count * ROWS, width), jnp.float32),
            pltpu.VMEM((term_count * ROWS, width), jnp.bfloat16),
            pltpu.VMEM((term_count * ROWS, width), jnp.bfloat16),
            pltpu.VMEM((term_count * ROWS, BLOCK), jnp.float32),
        ],
    )(mask, band, *operands)


def split_up(x, dim, count):
    shape = x.shape
    tiles = x.reshape(*shape[:dim], count, shape[dim] // count, *shape[dim + 1 :])
    return jnp.moveaxis(tiles, dim, 0)


def laid_out(tiles, dim):
    shape = list(tiles.shape[1:])
    shape[dim] *= tiles.shape[0]
    return jnp.moveaxis(tiles, 0, dim).reshape(shape)


def one_exchange(x, axis, axes, splits, concats):
    sizes = [lax.axis_size(a) for a in axes]
    tiles = split_up(x, splits[0], sizes[0])
    tiles = jnp.moveaxis(split_up(tiles, splits[1] + 1, sizes[1]), 0, 1)
    inside = tiles.shape[2:]
    tiles = tiles.reshape(-1, *inside)
    tiles = lax.all_to_all(tiles, axis, split_axis=0, concat_axis=0, tiled=True)
    tiles = laid_out(tiles.reshape(*sizes, *inside), concats[0] + 1)
    return laid_out(tiles, concats[1])


def extended_2(x, sides, width):
    edges = {}
    for axis, dim in sides:
        count, length = (lax.axis_size(axis), x.shape[dim])
        up = [(i, (i + 1) % count) for i in range(count - 1)]
        last = lax.slice_in_dim(x, length - width, length, axis=dim)
        first = lax.slice_in_dim(x, 0, width, axis=dim)
        edges[dim] = (
            lax.ppermute(last, axis, up),
            lax.ppermute(first, axis, [(b, a) for a, b in up]),
        )
    done = []
    for _, dim in sides:
        low, high = edges[dim]
        around = [(width, width) if d in done else (0, 0) for d in range(x.ndim)]
        x = jnp.concatenate([jnp.pad(low, around), x, jnp.pad(high, around)], axis=dim)
        done.append(dim)
    return x


def dft_table(length, direction):
    counter = jnp.arange(length, dtype=jnp.int32)
    product = counter[:, None] * counter[None, :] % length
    angles = product.astype(jnp.float32) * (direction * 2.0 * math.pi / length)
    cosine = jnp.cos(angles)
    sine_part = jnp.sin(angles)
    return jnp.stack([jnp.stack([cosine, -sine_part]), jnp.stack([sine_part, cosine])])


def twiddle(outer_size, inner_size, direction):
    product = (
        jnp.arange(outer_size, dtype=jnp.int32)[:, None]
        * jnp.arange(inner_size, dtype=jnp.int32)[None, :]
        % (outer_size * inner_size)
    )
    angles = product.astype(jnp.float32) * (direction * 2.0 * math.pi / (outer_size * inner_size))
    return (jnp.cos(angles), jnp.sin(angles))


def rotate(values, cosine, sine_part):
    return jnp.stack(
        [values[0] * cosine - values[1] * sine_part, values[0] * sine_part + values[1] * cosine]
    )


def spectral_core(values, phases):
    outer_size = values.shape[-2]
    inner_size = values.shape[-1]
    values = jnp.einsum("pqkn,q...nm->p...km", dft_table(outer_size, -1), values, precision=HIGHEST)
    cos_part, sin_part = twiddle(outer_size, inner_size, -1)
    values = rotate(values, cos_part, sin_part)
    values = jnp.einsum("pqjm,q...km->p...kj", dft_table(inner_size, -1), values, precision=HIGHEST)
    phase_grid = phases.reshape(inner_size, outer_size).T
    values = rotate(values, jnp.cos(phase_grid), jnp.sin(phase_grid))
    values = jnp.einsum("pqmj,q...kj->p...km", dft_table(inner_size, 1), values, precision=HIGHEST)
    cos_part, sin_part = twiddle(outer_size, inner_size, 1)
    return rotate(values, cos_part, sin_part)


def azimuth_compress(values, phases):
    length = values.shape[-1]
    inner_size = 128
    outer_size = length // inner_size
    spectrum = spectral_core(values.reshape(values.shape[:-1] + (outer_size, inner_size)), phases)
    result = (
        jnp.einsum("pqnk,q...km->p...nm", dft_table(outer_size, 1), spectrum, precision=HIGHEST)
        / length
    )
    return result.reshape(values.shape)


def range_compress(values, phases, row_count):
    length = values.shape[-1]
    inner_size = 128
    outer_size = length // inner_size
    spectrum = spectral_core(values.reshape(values.shape[:-1] + (outer_size, inner_size)), phases)
    inverse_rows = dft_table(outer_size, 1)
    result = jnp.einsum("pqnk,qdlkm->pdnml", inverse_rows, spectrum, precision=HIGHEST) / length
    return result.reshape(2, values.shape[1], row_count * inner_size, values.shape[2])


def range_blocks(values, phases):
    length = values.shape[-1]
    inner_size = 128
    outer_size = length // inner_size
    spectrum = spectral_core(values.reshape(values.shape[:-1] + (outer_size, inner_size)), phases)
    inverse_rows = dft_table(outer_size, 1)
    return jnp.einsum("pqnk,qdlkm->nmpdl", inverse_rows, spectrum, precision=HIGHEST) / length


def running_window(values):
    width = 2 * WIN_HALF + 1
    count = values.shape[-1]
    level = jnp.pad(values, ((0, 0), (0, 0), (WIN_HALF, WIN_HALF)))
    total = jnp.zeros_like(values)
    offset = 0
    span = 1
    while span <= width:
        if width & span:
            total = total + level[..., offset : offset + count]
            offset = offset + span
        level = level[..., :-span] + level[..., span:]
        span = span * 2
    return total


def link_block(real_ext, imag_ext, valid_mask):
    date_count = real_ext.shape[0]
    pair_list = [
        (former, latter) for former in range(date_count) for latter in range(former + 1, date_count)
    ]
    terms = [
        real_ext[former] * real_ext[former] + imag_ext[former] * imag_ext[former]
        for former in range(date_count)
    ]
    for former, latter in pair_list:
        terms.append(real_ext[former] * real_ext[latter] + imag_ext[former] * imag_ext[latter])
        terms.append(imag_ext[former] * real_ext[latter] - real_ext[former] * imag_ext[latter])
    stacked = jnp.stack(terms)
    across = stacked[:, :-2] + stacked[:, 1:-1] + stacked[:, 2:]
    window = running_window(across)
    window = window / (3 * (2 * WIN_HALF + 1))
    powers = window[:date_count] + 1e-06
    coherence = {}
    for number, pair in enumerate(pair_list):
        factor = lax.rsqrt(powers[pair[0]] * powers[pair[1]])
        coherence[pair] = (
            window[date_count + 2 * number] * factor,
            window[date_count + 2 * number + 1] * factor,
        )
    vector_real = [jnp.ones_like(powers[0]) for former in range(date_count)]
    vector_imag = [jnp.zeros_like(powers[0]) for former in range(date_count)]
    for iteration in range(POWER_ITERS):
        new_real = []
        new_imag = []
        for target in range(date_count):
            acc_real = vector_real[target]
            acc_imag = vector_imag[target]
            for source in range(date_count):
                if source != target:
                    if target < source:
                        part_real, part_imag = coherence[target, source]
                    else:
                        part_real, part_imag = coherence[source, target]
                        part_imag = -part_imag
                    acc_real = (
                        acc_real + part_real * vector_real[source] - part_imag * vector_imag[source]
                    )
                    acc_imag = (
                        acc_imag + part_real * vector_imag[source] + part_imag * vector_real[source]
                    )
            new_real.append(acc_real)
            new_imag.append(acc_imag)
        mean_square = (
            sum(
                (
                    new_real[target] * new_real[target] + new_imag[target] * new_imag[target]
                    for target in range(date_count)
                )
            )
            / date_count
        )
        factor = lax.rsqrt(jnp.maximum(mean_square, 1.0))
        vector_real = [entry * factor for entry in new_real]
        vector_imag = [entry * factor for entry in new_imag]
    magnitude = sum(
        (
            jnp.sqrt(
                coherence[pair][0] * coherence[pair][0] + coherence[pair][1] * coherence[pair][1]
            )
            for pair in pair_list
        )
    ) / len(pair_list)
    quality = valid_mask[:, None] * (0.05 + magnitude)
    vector = jnp.stack([jnp.stack(vector_real), jnp.stack(vector_imag)])
    return (vector, quality)


def shards(raw_echoes, range_phase, azimuth_phase, calibration):
    groups = lax.axis_size("date")
    group_dates = raw_echoes.shape[1]
    local_lines = raw_echoes.shape[2]
    length = raw_echoes.shape[3]
    outer_size = length // 128
    devices = groups * lax.axis_size("strip")
    ranged = range_blocks(raw_echoes.astype(jnp.float32), range_phase)
    tiles = ranged.reshape(devices, -1, 128)
    tiles = lax.all_to_all(tiles, ("date", "strip"), 0, 0, tiled=True)
    strips = devices // groups
    block_range = length // devices
    received = tiles.reshape(groups, strips, block_range, 2, group_dates, local_lines)
    turned = received.transpose(3, 0, 4, 2, 1, 5).reshape(
        2, groups * group_dates, block_range, strips * local_lines
    )
    focused = azimuth_compress(turned, azimuth_phase)
    all_dates = group_dates * groups
    column_count = calibration.shape[1]
    line_count = focused.shape[-1]
    image = focused.reshape(2, all_dates, column_count, line_count) * calibration[None, :, :, None]
    halo = 1 + SMOOTH_PASSES
    axes = ("date", "strip")
    count = lax.axis_size("date") * lax.axis_size("strip")
    up = [(i, i + 1) for i in range(count - 1)]
    edge_shape = (-1, line_count)
    low = lax.ppermute(image[:, :, column_count - halo :].reshape(edge_shape), axes, up)
    high = lax.ppermute(image[:, :, :halo].reshape(edge_shape), axes, [(b, a) for a, b in up])
    total_columns = column_count * lax.axis_size("date") * lax.axis_size("strip")
    first = lax.axis_index(("date", "strip")) * column_count - SMOOTH_PASSES
    columns = first + jnp.arange(column_count + 2 * SMOOTH_PASSES, dtype=jnp.int32)
    valid_mask = ((columns >= 0) & (columns < total_columns)).astype(jnp.float32)
    vector, quality = link_and_smooth((low, image, high), valid_mask)
    return (vector, quality)


def solution(mesh):
    in_specs = (P(None, "date", "strip", None), P(), P(), P(None, ("date", "strip")))
    out_specs = (P(None, None, ("date", "strip"), None), P(("date", "strip"), None))
    return jax.shard_map(shards, mesh=mesh, in_specs=in_specs, out_specs=out_specs, check_vma=False)
```

```python
import math

import numpy as np

import jax
import jax.numpy as jnp
from jax import lax
from jax.experimental import pallas as pl
from jax.experimental.pallas import tpu as pltpu
from jax.sharding import PartitionSpec as P

WIN_HALF = 11
POWER_ITERS = 6
SMOOTH_PASSES = 2


DFT_PRECISION = lax.Precision.HIGH
BLOCK = 2048
EDGE = 128
CHUNK = 128
ROWS = 8


def link_kernel(mask_ref, band_ref, *refs):
    pieces = refs[:9]
    vec_ref, qual_ref, image, terms, high, low, sums = refs[9:]
    step = pl.program_id(0)
    last = pl.num_programs(0) - 1
    dates = pieces[4].shape[1]
    block = pieces[4].shape[3]
    padded = image.shape[2]
    row = 0
    for number in range(3):
        prev_ref, cur_ref, next_ref = pieces[3 * number : 3 * number + 3]
        if len(cur_ref.shape) == 4:
            count = cur_ref.shape[2]
            rows = slice(row, row + count)
            image[:, :, rows, EDGE : EDGE + block] = cur_ref[...]
            image[:, :, rows, :EDGE] = jnp.where(step > 0, prev_ref[...], 0.0)
            image[:, :, rows, EDGE + block :] = jnp.where(step < last, next_ref[...], 0.0)
        else:
            count = cur_ref.shape[0] // (image.shape[0] * dates)
            rows = slice(row, row + count)
            for p in range(image.shape[0]):
                for d in range(dates):
                    source = slice((p * dates + d) * count, (p * dates + d + 1) * count)
                    image[p, d, rows, EDGE : EDGE + block] = cur_ref[source, :]
                    image[p, d, rows, :EDGE] = jnp.where(step > 0, prev_ref[source, :], 0.0)
                    image[p, d, rows, EDGE + block :] = jnp.where(step < last, next_ref[source, :], 0.0)
        row += count
    image[:, :, row:, :] = jnp.zeros((image.shape[0], dates, padded - row, image.shape[3]), jnp.float32)
    pairs = [(a, b) for a in range(dates) for b in range(a + 1, dates)]
    specs = [(0, a, a) for a in range(dates)]
    for a, b in pairs:
        specs.append((1, a, b))
        specs.append((2, a, b))

    for number, (kind, a, b) in enumerate(specs):
        ra, ia = image[0, a], image[1, a]
        if kind == 0:
            value = ra * ra + ia * ia
        else:
            rb, ib = image[0, b], image[1, b]
            if kind == 1:
                value = ra * rb + ia * ib
            else:
                value = ia * rb - ra * ib
        across = value + pltpu.roll(value, padded - 1, 0) + pltpu.roll(value, padded - 2, 0)
        terms[number * ROWS : (number + 1) * ROWS, :] = across[:ROWS]
    full = terms[...]
    top = full.astype(jnp.bfloat16)
    high[...] = top
    low[...] = (full - top.astype(jnp.float32)).astype(jnp.bfloat16)
    band = band_ref[...]
    for index in range(block // CHUNK):
        left = index * CHUNK
        window = jnp.dot(high[:, left : left + CHUNK + 2 * EDGE], band, preferred_element_type=jnp.float32)
        window = window + jnp.dot(low[:, left : left + CHUNK + 2 * EDGE], band, preferred_element_type=jnp.float32)
        sums[:, left : left + CHUNK] = window

    mask = mask_ref[...]
    inverse_scale = 1.0 / (3 * (2 * WIN_HALF + 1))

    def chunk_body(index, carry):
        start = pl.multiple_of(index * CHUNK, CHUNK)
        window = [
            sums[number * ROWS : (number + 1) * ROWS, pl.ds(start, CHUNK)] * inverse_scale
            for number in range(len(specs))
        ]
        powers = [window[a] + 1e-06 for a in range(dates)]
        coherence = {}
        for number, (a, b) in enumerate(pairs):
            factor = lax.rsqrt(powers[a] * powers[b])
            coherence[a, b] = (
                window[dates + 2 * number] * factor,
                window[dates + 2 * number + 1] * factor,
            )

        def entry(target, source):
            if target < source:
                return coherence[target, source]
            part_real, part_imag = coherence[source, target]
            return part_real, -part_imag

        new_real = []
        new_imag = []
        for target in range(dates):
            sources = [entry(target, source) for source in range(dates) if source != target]
            new_real.append(1.0 + sum(part[0] for part in sources))
            new_imag.append(sum(part[1] for part in sources))
        for iteration in range(POWER_ITERS):
            if iteration > 0:
                new_real = []
                new_imag = []
                for target in range(dates):
                    acc_real = vector_real[target]
                    acc_imag = vector_imag[target]
                    for source in range(dates):
                        if source != target:
                            part_real, part_imag = entry(target, source)
                            acc_real = (
                                acc_real + part_real * vector_real[source] - part_imag * vector_imag[source]
                            )
                            acc_imag = (
                                acc_imag + part_real * vector_imag[source] + part_imag * vector_real[source]
                            )
                    new_real.append(acc_real)
                    new_imag.append(acc_imag)
            mean_square = (
                sum(new_real[t] * new_real[t] + new_imag[t] * new_imag[t] for t in range(dates)) / dates
            )
            factor = lax.rsqrt(jnp.maximum(mean_square, 1.0))
            vector_real = [value * factor for value in new_real]
            vector_imag = [value * factor for value in new_imag]
        magnitude = sum(
            jnp.sqrt(coherence[pair][0] * coherence[pair][0] + coherence[pair][1] * coherence[pair][1])
            for pair in pairs
        ) / len(pairs)
        quality = mask * (0.05 + magnitude)
        vectors = vector_real + vector_imag
        for passes in range(SMOOTH_PASSES):
            denominator = quality + pltpu.roll(quality, 1, 0) + pltpu.roll(quality, ROWS - 1, 0)
            inverse = 1.0 / jnp.where(denominator > 0, denominator, 1.0)
            smoothed = []
            for value in vectors:
                weighted = value * quality
                numerator = weighted + pltpu.roll(weighted, 1, 0) + pltpu.roll(weighted, ROWS - 1, 0)
                smoothed.append(numerator * inverse)
            vectors = smoothed
        keep = slice(SMOOTH_PASSES, ROWS - SMOOTH_PASSES)
        for number, value in enumerate(vectors):
            vec_ref[number // dates, number % dates, :, pl.ds(start, CHUNK)] = value[keep]
        qual_ref[:, pl.ds(start, CHUNK)] = quality[keep]
        return carry

    lax.fori_loop(0, block // CHUNK, chunk_body, 0)


def link_and_smooth(pieces, valid_mask):
    parts, dates, _, lines = pieces[1].shape
    assert all(piece.shape[-1] == lines for piece in pieces)
    padded = 16
    kept = ROWS - 2 * SMOOTH_PASSES
    steps = lines // BLOCK
    per_block = BLOCK // EDGE
    edges = lines // EDGE
    term_count = dates + dates * (dates - 1)
    mask = jnp.broadcast_to(valid_mask[:, None], (ROWS, CHUNK))
    offset = np.arange(CHUNK + 2 * EDGE)[:, None] - EDGE - np.arange(CHUNK)[None, :]
    band = jnp.asarray(np.abs(offset) <= WIN_HALF, jnp.bfloat16)
    width = BLOCK + 2 * EDGE
    piece_specs = []
    operands = []
    for piece in pieces:
        lead = (0,) * (piece.ndim - 1)
        piece_specs += [
            pl.BlockSpec(piece.shape[:-1] + (EDGE,), lambda i, lead=lead: lead + (jnp.maximum(i * per_block - 1, 0),)),
            pl.BlockSpec(piece.shape[:-1] + (BLOCK,), lambda i, lead=lead: lead + (i,)),
            pl.BlockSpec(piece.shape[:-1] + (EDGE,), lambda i, lead=lead: lead + (jnp.minimum((i + 1) * per_block, edges - 1),)),
        ]
        operands += [piece, piece, piece]
    return pl.pallas_call(
        link_kernel,
        grid=(steps,),
        in_specs=[
            pl.BlockSpec((ROWS, CHUNK), lambda i: (0, 0)),
            pl.BlockSpec((CHUNK + 2 * EDGE, CHUNK), lambda i: (0, 0)),
        ]
        + piece_specs,
        out_specs=[
            pl.BlockSpec((parts, dates, kept, BLOCK), lambda i: (0, 0, 0, i)),
            pl.BlockSpec((kept, BLOCK), lambda i: (0, i)),
        ],
        out_shape=[
            jax.ShapeDtypeStruct((parts, dates, kept, lines), jnp.float32),
            jax.ShapeDtypeStruct((kept, lines), jnp.float32),
        ],
        scratch_shapes=[
            pltpu.VMEM((parts, dates, padded, width), jnp.float32),
            pltpu.VMEM((term_count * ROWS, width), jnp.float32),
            pltpu.VMEM((term_count * ROWS, width), jnp.bfloat16),
            pltpu.VMEM((term_count * ROWS, width), jnp.bfloat16),
            pltpu.VMEM((term_count * ROWS, BLOCK), jnp.float32),
        ],
    )(mask, band, *operands)


def split_up(x, dim, count):
    shape = x.shape
    tiles = x.reshape(*shape[:dim], count, shape[dim] // count, *shape[dim + 1 :])
    return jnp.moveaxis(tiles, dim, 0)


def laid_out(tiles, dim):
    shape = list(tiles.shape[1:])
    shape[dim] *= tiles.shape[0]
    return jnp.moveaxis(tiles, 0, dim).reshape(shape)


def one_exchange(x, axis, axes, splits, concats):
    sizes = [lax.axis_size(a) for a in axes]
    tiles = split_up(x, splits[0], sizes[0])
    tiles = jnp.moveaxis(split_up(tiles, splits[1] + 1, sizes[1]), 0, 1)
    inside = tiles.shape[2:]
    tiles = tiles.reshape(-1, *inside)
    tiles = lax.all_to_all(tiles, axis, split_axis=0, concat_axis=0, tiled=True)
    tiles = laid_out(tiles.reshape(*sizes, *inside), concats[0] + 1)
    return laid_out(tiles, concats[1])


def extended_2(x, sides, width):
    edges = {}
    for axis, dim in sides:
        count, length = (lax.axis_size(axis), x.shape[dim])
        up = [(i, (i + 1) % count) for i in range(count - 1)]
        last = lax.slice_in_dim(x, length - width, length, axis=dim)
        first = lax.slice_in_dim(x, 0, width, axis=dim)
        edges[dim] = (
            lax.ppermute(last, axis, up),
            lax.ppermute(first, axis, [(b, a) for a, b in up]),
        )
    done = []
    for _, dim in sides:
        low, high = edges[dim]
        around = [(width, width) if d in done else (0, 0) for d in range(x.ndim)]
        x = jnp.concatenate([jnp.pad(low, around), x, jnp.pad(high, around)], axis=dim)
        done.append(dim)
    return x


def dft_table(length, direction):
    counter = jnp.arange(length, dtype=jnp.int32)
    product = counter[:, None] * counter[None, :] % length
    angles = product.astype(jnp.float32) * (direction * 2.0 * math.pi / length)
    cosine = jnp.cos(angles)
    sine_part = jnp.sin(angles)
    return jnp.stack([jnp.stack([cosine, -sine_part]), jnp.stack([sine_part, cosine])])


def twiddle(outer_size, inner_size, direction):
    product = (
        jnp.arange(outer_size, dtype=jnp.int32)[:, None]
        * jnp.arange(inner_size, dtype=jnp.int32)[None, :]
        % (outer_size * inner_size)
    )
    angles = product.astype(jnp.float32) * (direction * 2.0 * math.pi / (outer_size * inner_size))
    return (jnp.cos(angles), jnp.sin(angles))


def rotate(values, cosine, sine_part):
    return jnp.stack(
        [values[0] * cosine - values[1] * sine_part, values[0] * sine_part + values[1] * cosine]
    )


def spectral_core(values, phases):
    outer_size = values.shape[-2]
    inner_size = values.shape[-1]
    values = jnp.einsum("pqkn,q...nm->p...km", dft_table(outer_size, -1), values, precision=DFT_PRECISION)
    cos_part, sin_part = twiddle(outer_size, inner_size, -1)
    values = rotate(values, cos_part, sin_part)
    values = jnp.einsum("pqjm,q...km->p...kj", dft_table(inner_size, -1), values, precision=DFT_PRECISION)
    phase_grid = phases.reshape(inner_size, outer_size).T
    values = rotate(values, jnp.cos(phase_grid), jnp.sin(phase_grid))
    values = jnp.einsum("pqmj,q...kj->p...km", dft_table(inner_size, 1), values, precision=DFT_PRECISION)
    cos_part, sin_part = twiddle(outer_size, inner_size, 1)
    return rotate(values, cos_part, sin_part)


def azimuth_compress(values, phases):
    length = values.shape[-1]
    inner_size = 128
    outer_size = length // inner_size
    spectrum = spectral_core(values.reshape(values.shape[:-1] + (outer_size, inner_size)), phases)
    result = (
        jnp.einsum("pqnk,q...km->p...nm", dft_table(outer_size, 1), spectrum, precision=DFT_PRECISION)
        / length
    )
    return result.reshape(values.shape)


def range_compress(values, phases, row_count):
    length = values.shape[-1]
    inner_size = 128
    outer_size = length // inner_size
    spectrum = spectral_core(values.reshape(values.shape[:-1] + (outer_size, inner_size)), phases)
    inverse_rows = dft_table(outer_size, 1)
    result = jnp.einsum("pqnk,qdlkm->pdnml", inverse_rows, spectrum, precision=DFT_PRECISION) / length
    return result.reshape(2, values.shape[1], row_count * inner_size, values.shape[2])


def range_blocks(values, phases):
    length = values.shape[-1]
    inner_size = 128
    outer_size = length // inner_size
    spectrum = spectral_core(values.reshape(values.shape[:-1] + (outer_size, inner_size)), phases)
    inverse_rows = dft_table(outer_size, 1)
    return jnp.einsum("pqnk,qdlkm->nmpdl", inverse_rows, spectrum, precision=DFT_PRECISION) / length


def running_window(values):
    width = 2 * WIN_HALF + 1
    count = values.shape[-1]
    level = jnp.pad(values, ((0, 0), (0, 0), (WIN_HALF, WIN_HALF)))
    total = jnp.zeros_like(values)
    offset = 0
    span = 1
    while span <= width:
        if width & span:
            total = total + level[..., offset : offset + count]
            offset = offset + span
        level = level[..., :-span] + level[..., span:]
        span = span * 2
    return total


def link_block(real_ext, imag_ext, valid_mask):
    date_count = real_ext.shape[0]
    pair_list = [
        (former, latter) for former in range(date_count) for latter in range(former + 1, date_count)
    ]
    terms = [
        real_ext[former] * real_ext[former] + imag_ext[former] * imag_ext[former]
        for former in range(date_count)
    ]
    for former, latter in pair_list:
        terms.append(real_ext[former] * real_ext[latter] + imag_ext[former] * imag_ext[latter])
        terms.append(imag_ext[former] * real_ext[latter] - real_ext[former] * imag_ext[latter])
    stacked = jnp.stack(terms)
    across = stacked[:, :-2] + stacked[:, 1:-1] + stacked[:, 2:]
    window = running_window(across)
    window = window / (3 * (2 * WIN_HALF + 1))
    powers = window[:date_count] + 1e-06
    coherence = {}
    for number, pair in enumerate(pair_list):
        factor = lax.rsqrt(powers[pair[0]] * powers[pair[1]])
        coherence[pair] = (
            window[date_count + 2 * number] * factor,
            window[date_count + 2 * number + 1] * factor,
        )
    vector_real = [jnp.ones_like(powers[0]) for former in range(date_count)]
    vector_imag = [jnp.zeros_like(powers[0]) for former in range(date_count)]
    for iteration in range(POWER_ITERS):
        new_real = []
        new_imag = []
        for target in range(date_count):
            acc_real = vector_real[target]
            acc_imag = vector_imag[target]
            for source in range(date_count):
                if source != target:
                    if target < source:
                        part_real, part_imag = coherence[target, source]
                    else:
                        part_real, part_imag = coherence[source, target]
                        part_imag = -part_imag
                    acc_real = (
                        acc_real + part_real * vector_real[source] - part_imag * vector_imag[source]
                    )
                    acc_imag = (
                        acc_imag + part_real * vector_imag[source] + part_imag * vector_real[source]
                    )
            new_real.append(acc_real)
            new_imag.append(acc_imag)
        mean_square = (
            sum(
                (
                    new_real[target] * new_real[target] + new_imag[target] * new_imag[target]
                    for target in range(date_count)
                )
            )
            / date_count
        )
        factor = lax.rsqrt(jnp.maximum(mean_square, 1.0))
        vector_real = [entry * factor for entry in new_real]
        vector_imag = [entry * factor for entry in new_imag]
    magnitude = sum(
        (
            jnp.sqrt(
                coherence[pair][0] * coherence[pair][0] + coherence[pair][1] * coherence[pair][1]
            )
            for pair in pair_list
        )
    ) / len(pair_list)
    quality = valid_mask[:, None] * (0.05 + magnitude)
    vector = jnp.stack([jnp.stack(vector_real), jnp.stack(vector_imag)])
    return (vector, quality)


def shards(raw_echoes, range_phase, azimuth_phase, calibration):
    groups = lax.axis_size("date")
    group_dates = raw_echoes.shape[1]
    local_lines = raw_echoes.shape[2]
    length = raw_echoes.shape[3]
    outer_size = length // 128
    devices = groups * lax.axis_size("strip")
    ranged = range_blocks(raw_echoes.astype(jnp.float32), range_phase)
    tiles = ranged.reshape(devices, -1, 128)
    tiles = lax.all_to_all(tiles, ("date", "strip"), 0, 0, tiled=True)
    strips = devices // groups
    block_range = length // devices
    received = tiles.reshape(groups, strips, block_range, 2, group_dates, local_lines)
    turned = received.transpose(3, 0, 4, 2, 1, 5).reshape(
        2, groups * group_dates, block_range, strips * local_lines
    )
    focused = azimuth_compress(turned, azimuth_phase)
    all_dates = group_dates * groups
    column_count = calibration.shape[1]
    line_count = focused.shape[-1]
    image = focused.reshape(2, all_dates, column_count, line_count) * calibration[None, :, :, None]
    halo = 1 + SMOOTH_PASSES
    axes = ("date", "strip")
    count = lax.axis_size("date") * lax.axis_size("strip")
    up = [(i, i + 1) for i in range(count - 1)]
    edge_shape = (-1, line_count)
    low = lax.ppermute(image[:, :, column_count - halo :].reshape(edge_shape), axes, up)
    high = lax.ppermute(image[:, :, :halo].reshape(edge_shape), axes, [(b, a) for a, b in up])
    total_columns = column_count * lax.axis_size("date") * lax.axis_size("strip")
    first = lax.axis_index(("date", "strip")) * column_count - SMOOTH_PASSES
    columns = first + jnp.arange(column_count + 2 * SMOOTH_PASSES, dtype=jnp.int32)
    valid_mask = ((columns >= 0) & (columns < total_columns)).astype(jnp.float32)
    vector, quality = link_and_smooth((low, image, high), valid_mask)
    return (vector, quality)


def solution(mesh):
    in_specs = (P(None, "date", "strip", None), P(), P(), P(None, ("date", "strip")))
    out_specs = (P(None, None, ("date", "strip"), None), P(("date", "strip"), None))
    return jax.shard_map(shards, mesh=mesh, in_specs=in_specs, out_specs=out_specs, check_vma=False)
```

```python
import math

import numpy as np

import jax
import jax.numpy as jnp
from jax import lax
from jax.experimental import pallas as pl
from jax.experimental.pallas import tpu as pltpu
from jax.sharding import PartitionSpec as P

WIN_HALF = 11
POWER_ITERS = 6
SMOOTH_PASSES = 2


DFT_PRECISION = lax.Precision.HIGH
BLOCK = 2048
EDGE = 128
CHUNK = 128
ROWS = 8


def link_kernel(mask_ref, band_ref, *refs):
    pieces = refs[:9]
    vec_ref, qual_ref, image, high, low, sums = refs[9:]
    step = pl.program_id(0)
    last = pl.num_programs(0) - 1
    dates = pieces[4].shape[1]
    block = pieces[4].shape[3]
    padded = image.shape[2]
    row = 0
    for number in range(3):
        prev_ref, cur_ref, next_ref = pieces[3 * number : 3 * number + 3]
        if len(cur_ref.shape) == 4:
            count = cur_ref.shape[2]
            rows = slice(row, row + count)
            image[:, :, rows, EDGE : EDGE + block] = cur_ref[...]
            image[:, :, rows, :EDGE] = jnp.where(step > 0, prev_ref[...], 0.0)
            image[:, :, rows, EDGE + block :] = jnp.where(step < last, next_ref[...], 0.0)
        else:
            count = cur_ref.shape[0] // (image.shape[0] * dates)
            rows = slice(row, row + count)
            for p in range(image.shape[0]):
                for d in range(dates):
                    source = slice((p * dates + d) * count, (p * dates + d + 1) * count)
                    image[p, d, rows, EDGE : EDGE + block] = cur_ref[source, :]
                    image[p, d, rows, :EDGE] = jnp.where(step > 0, prev_ref[source, :], 0.0)
                    image[p, d, rows, EDGE + block :] = jnp.where(step < last, next_ref[source, :], 0.0)
        row += count
    image[:, :, row:, :] = jnp.zeros((image.shape[0], dates, padded - row, image.shape[3]), jnp.float32)
    pairs = [(a, b) for a in range(dates) for b in range(a + 1, dates)]
    specs = [(0, a, a) for a in range(dates)]
    for a, b in pairs:
        specs.append((1, a, b))
        specs.append((2, a, b))

    def product(kind, a, b, rows, lanes):
        ra, ia = image[0, a, rows, lanes], image[1, a, rows, lanes]
        if kind == 0:
            return ra * ra + ia * ia
        rb, ib = image[0, b, rows, lanes], image[1, b, rows, lanes]
        if kind == 1:
            return ra * rb + ia * ib
        return ia * rb - ra * ib

    row_index = lax.broadcasted_iota(jnp.int32, (ROWS, CHUNK), 0)

    def term_body(column):
        lanes = slice(column * CHUNK, (column + 1) * CHUNK)
        sums_of_pair = []
        for number, (kind, a, b) in enumerate(specs):
            upper = product(kind, a, b, slice(0, ROWS), lanes)
            lower = product(kind, a, b, slice(ROWS, 2 * ROWS), lanes)
            one = jnp.where(row_index < ROWS - 1, pltpu.roll(upper, ROWS - 1, 0), pltpu.roll(lower, ROWS - 1, 0))
            two = jnp.where(row_index < ROWS - 2, pltpu.roll(upper, ROWS - 2, 0), pltpu.roll(lower, ROWS - 2, 0))
            sums_of_pair.append(upper + one + two)
            if len(sums_of_pair) == 2:
                full = jnp.concatenate(sums_of_pair, axis=0)
                top = full.astype(jnp.bfloat16)
                rows = slice((number - 1) * ROWS, (number + 1) * ROWS)
                high[rows, lanes] = top
                low[rows, lanes] = (full - top.astype(jnp.float32)).astype(jnp.bfloat16)
                sums_of_pair = []

        if column >= 2:
            left = (column - 2) * CHUNK
            window = jnp.dot(high[:, left : left + CHUNK + 2 * EDGE], band, preferred_element_type=jnp.float32)
            window = window + jnp.dot(
                low[:, left : left + CHUNK + 2 * EDGE], band, preferred_element_type=jnp.float32
            )
            sums[:, left : left + CHUNK] = window

    band = band_ref[...]
    for column in range(image.shape[3] // CHUNK):
        term_body(column)
    mask = mask_ref[...]
    inverse_scale = 1.0 / (3 * (2 * WIN_HALF + 1))

    def chunk_body(index, carry):
        start = pl.multiple_of(index * CHUNK, CHUNK)
        window = [
            sums[number * ROWS : (number + 1) * ROWS, pl.ds(start, CHUNK)] * inverse_scale
            for number in range(len(specs))
        ]
        powers = [window[a] + 1e-06 for a in range(dates)]
        coherence = {}
        for number, (a, b) in enumerate(pairs):
            factor = lax.rsqrt(powers[a] * powers[b])
            coherence[a, b] = (
                window[dates + 2 * number] * factor,
                window[dates + 2 * number + 1] * factor,
            )

        def entry(target, source):
            if target < source:
                return coherence[target, source]
            part_real, part_imag = coherence[source, target]
            return part_real, -part_imag

        new_real = []
        new_imag = []
        for target in range(dates):
            sources = [entry(target, source) for source in range(dates) if source != target]
            new_real.append(1.0 + sum(part[0] for part in sources))
            new_imag.append(sum(part[1] for part in sources))
        for iteration in range(POWER_ITERS):
            if iteration > 0:
                new_real = []
                new_imag = []
                for target in range(dates):
                    acc_real = vector_real[target]
                    acc_imag = vector_imag[target]
                    for source in range(dates):
                        if source != target:
                            part_real, part_imag = entry(target, source)
                            acc_real = (
                                acc_real + part_real * vector_real[source] - part_imag * vector_imag[source]
                            )
                            acc_imag = (
                                acc_imag + part_real * vector_imag[source] + part_imag * vector_real[source]
                            )
                    new_real.append(acc_real)
                    new_imag.append(acc_imag)
            mean_square = (
                sum(new_real[t] * new_real[t] + new_imag[t] * new_imag[t] for t in range(dates)) / dates
            )
            factor = lax.rsqrt(jnp.maximum(mean_square, 1.0))
            vector_real = [value * factor for value in new_real]
            vector_imag = [value * factor for value in new_imag]
        magnitude = sum(
            jnp.sqrt(coherence[pair][0] * coherence[pair][0] + coherence[pair][1] * coherence[pair][1])
            for pair in pairs
        ) / len(pairs)
        quality = mask * (0.05 + magnitude)
        vectors = vector_real + vector_imag
        for passes in range(SMOOTH_PASSES):
            denominator = quality + pltpu.roll(quality, 1, 0) + pltpu.roll(quality, ROWS - 1, 0)
            inverse = 1.0 / jnp.where(denominator > 0, denominator, 1.0)
            smoothed = []
            for value in vectors:
                weighted = value * quality
                numerator = weighted + pltpu.roll(weighted, 1, 0) + pltpu.roll(weighted, ROWS - 1, 0)
                smoothed.append(numerator * inverse)
            vectors = smoothed
        keep = slice(SMOOTH_PASSES, ROWS - SMOOTH_PASSES)
        for number, value in enumerate(vectors):
            vec_ref[number // dates, number % dates, :, pl.ds(start, CHUNK)] = value[keep]
        qual_ref[:, pl.ds(start, CHUNK)] = quality[keep]
        return carry

    lax.fori_loop(0, block // CHUNK, chunk_body, 0, unroll=4)


def link_and_smooth(pieces, valid_mask):
    parts, dates, _, lines = pieces[1].shape
    assert all(piece.shape[-1] == lines for piece in pieces)
    padded = 16
    kept = ROWS - 2 * SMOOTH_PASSES
    steps = lines // BLOCK
    per_block = BLOCK // EDGE
    edges = lines // EDGE
    term_count = dates + dates * (dates - 1)
    mask = jnp.broadcast_to(valid_mask[:, None], (ROWS, CHUNK))
    offset = np.arange(CHUNK + 2 * EDGE)[:, None] - EDGE - np.arange(CHUNK)[None, :]
    band = jnp.asarray(np.abs(offset) <= WIN_HALF, jnp.bfloat16)
    width = BLOCK + 2 * EDGE
    piece_specs = []
    operands = []
    for piece in pieces:
        lead = (0,) * (piece.ndim - 1)
        piece_specs += [
            pl.BlockSpec(piece.shape[:-1] + (EDGE,), lambda i, lead=lead: lead + (jnp.maximum(i * per_block - 1, 0),)),
            pl.BlockSpec(piece.shape[:-1] + (BLOCK,), lambda i, lead=lead: lead + (i,)),
            pl.BlockSpec(piece.shape[:-1] + (EDGE,), lambda i, lead=lead: lead + (jnp.minimum((i + 1) * per_block, edges - 1),)),
        ]
        operands += [piece, piece, piece]
    return pl.pallas_call(
        link_kernel,
        grid=(steps,),
        in_specs=[
            pl.BlockSpec((ROWS, CHUNK), lambda i: (0, 0)),
            pl.BlockSpec((CHUNK + 2 * EDGE, CHUNK), lambda i: (0, 0)),
        ]
        + piece_specs,
        out_specs=[
            pl.BlockSpec((parts, dates, kept, BLOCK), lambda i: (0, 0, 0, i)),
            pl.BlockSpec((kept, BLOCK), lambda i: (0, i)),
        ],
        out_shape=[
            jax.ShapeDtypeStruct((parts, dates, kept, lines), jnp.float32),
            jax.ShapeDtypeStruct((kept, lines), jnp.float32),
        ],
        scratch_shapes=[
            pltpu.VMEM((parts, dates, padded, width), jnp.float32),
            pltpu.VMEM((term_count * ROWS, width), jnp.bfloat16),
            pltpu.VMEM((term_count * ROWS, width), jnp.bfloat16),
            pltpu.VMEM((term_count * ROWS, BLOCK), jnp.float32),
        ],
    )(mask, band, *operands)


def split_up(x, dim, count):
    shape = x.shape
    tiles = x.reshape(*shape[:dim], count, shape[dim] // count, *shape[dim + 1 :])
    return jnp.moveaxis(tiles, dim, 0)


def laid_out(tiles, dim):
    shape = list(tiles.shape[1:])
    shape[dim] *= tiles.shape[0]
    return jnp.moveaxis(tiles, 0, dim).reshape(shape)


def one_exchange(x, axis, axes, splits, concats):
    sizes = [lax.axis_size(a) for a in axes]
    tiles = split_up(x, splits[0], sizes[0])
    tiles = jnp.moveaxis(split_up(tiles, splits[1] + 1, sizes[1]), 0, 1)
    inside = tiles.shape[2:]
    tiles = tiles.reshape(-1, *inside)
    tiles = lax.all_to_all(tiles, axis, split_axis=0, concat_axis=0, tiled=True)
    tiles = laid_out(tiles.reshape(*sizes, *inside), concats[0] + 1)
    return laid_out(tiles, concats[1])


def extended_2(x, sides, width):
    edges = {}
    for axis, dim in sides:
        count, length = (lax.axis_size(axis), x.shape[dim])
        up = [(i, (i + 1) % count) for i in range(count - 1)]
        last = lax.slice_in_dim(x, length - width, length, axis=dim)
        first = lax.slice_in_dim(x, 0, width, axis=dim)
        edges[dim] = (
            lax.ppermute(last, axis, up),
            lax.ppermute(first, axis, [(b, a) for a, b in up]),
        )
    done = []
    for _, dim in sides:
        low, high = edges[dim]
        around = [(width, width) if d in done else (0, 0) for d in range(x.ndim)]
        x = jnp.concatenate([jnp.pad(low, around), x, jnp.pad(high, around)], axis=dim)
        done.append(dim)
    return x


def dft_table(length, direction):
    counter = jnp.arange(length, dtype=jnp.int32)
    product = counter[:, None] * counter[None, :] % length
    angles = product.astype(jnp.float32) * (direction * 2.0 * math.pi / length)
    cosine = jnp.cos(angles)
    sine_part = jnp.sin(angles)
    return jnp.stack([jnp.stack([cosine, -sine_part]), jnp.stack([sine_part, cosine])])


def twiddle(outer_size, inner_size, direction):
    product = (
        jnp.arange(outer_size, dtype=jnp.int32)[:, None]
        * jnp.arange(inner_size, dtype=jnp.int32)[None, :]
        % (outer_size * inner_size)
    )
    angles = product.astype(jnp.float32) * (direction * 2.0 * math.pi / (outer_size * inner_size))
    return (jnp.cos(angles), jnp.sin(angles))


def rotate(values, cosine, sine_part):
    return jnp.stack(
        [values[0] * cosine - values[1] * sine_part, values[0] * sine_part + values[1] * cosine]
    )


def spectral_core(values, phases):
    outer_size = values.shape[-2]
    inner_size = values.shape[-1]
    values = jnp.einsum("pqkn,q...nm->p...km", dft_table(outer_size, -1), values, precision=DFT_PRECISION)
    cos_part, sin_part = twiddle(outer_size, inner_size, -1)
    values = rotate(values, cos_part, sin_part)
    values = jnp.einsum("pqjm,q...km->p...kj", dft_table(inner_size, -1), values, precision=DFT_PRECISION)
    phase_grid = phases.reshape(inner_size, outer_size).T
    values = rotate(values, jnp.cos(phase_grid), jnp.sin(phase_grid))
    values = jnp.einsum("pqmj,q...kj->p...km", dft_table(inner_size, 1), values, precision=DFT_PRECISION)
    cos_part, sin_part = twiddle(outer_size, inner_size, 1)
    return rotate(values, cos_part, sin_part)


def azimuth_compress(values, phases):
    length = values.shape[-1]
    inner_size = 128
    outer_size = length // inner_size
    spectrum = spectral_core(values.reshape(values.shape[:-1] + (outer_size, inner_size)), phases)
    result = (
        jnp.einsum("pqnk,q...km->p...nm", dft_table(outer_size, 1), spectrum, precision=DFT_PRECISION)
        / length
    )
    return result.reshape(values.shape)


def range_compress(values, phases, row_count):
    length = values.shape[-1]
    inner_size = 128
    outer_size = length // inner_size
    spectrum = spectral_core(values.reshape(values.shape[:-1] + (outer_size, inner_size)), phases)
    inverse_rows = dft_table(outer_size, 1)
    result = jnp.einsum("pqnk,qdlkm->pdnml", inverse_rows, spectrum, precision=DFT_PRECISION) / length
    return result.reshape(2, values.shape[1], row_count * inner_size, values.shape[2])


def range_blocks(values, phases):
    length = values.shape[-1]
    inner_size = 128
    outer_size = length // inner_size
    spectrum = spectral_core(values.reshape(values.shape[:-1] + (outer_size, inner_size)), phases)
    inverse_rows = dft_table(outer_size, 1)
    return jnp.einsum("pqnk,qdlkm->nmpdl", inverse_rows, spectrum, precision=DFT_PRECISION) / length


def running_window(values):
    width = 2 * WIN_HALF + 1
    count = values.shape[-1]
    level = jnp.pad(values, ((0, 0), (0, 0), (WIN_HALF, WIN_HALF)))
    total = jnp.zeros_like(values)
    offset = 0
    span = 1
    while span <= width:
        if width & span:
            total = total + level[..., offset : offset + count]
            offset = offset + span
        level = level[..., :-span] + level[..., span:]
        span = span * 2
    return total


def link_block(real_ext, imag_ext, valid_mask):
    date_count = real_ext.shape[0]
    pair_list = [
        (former, latter) for former in range(date_count) for latter in range(former + 1, date_count)
    ]
    terms = [
        real_ext[former] * real_ext[former] + imag_ext[former] * imag_ext[former]
        for former in range(date_count)
    ]
    for former, latter in pair_list:
        terms.append(real_ext[former] * real_ext[latter] + imag_ext[former] * imag_ext[latter])
        terms.append(imag_ext[former] * real_ext[latter] - real_ext[former] * imag_ext[latter])
    stacked = jnp.stack(terms)
    across = stacked[:, :-2] + stacked[:, 1:-1] + stacked[:, 2:]
    window = running_window(across)
    window = window / (3 * (2 * WIN_HALF + 1))
    powers = window[:date_count] + 1e-06
    coherence = {}
    for number, pair in enumerate(pair_list):
        factor = lax.rsqrt(powers[pair[0]] * powers[pair[1]])
        coherence[pair] = (
            window[date_count + 2 * number] * factor,
            window[date_count + 2 * number + 1] * factor,
        )
    vector_real = [jnp.ones_like(powers[0]) for former in range(date_count)]
    vector_imag = [jnp.zeros_like(powers[0]) for former in range(date_count)]
    for iteration in range(POWER_ITERS):
        new_real = []
        new_imag = []
        for target in range(date_count):
            acc_real = vector_real[target]
            acc_imag = vector_imag[target]
            for source in range(date_count):
                if source != target:
                    if target < source:
                        part_real, part_imag = coherence[target, source]
                    else:
                        part_real, part_imag = coherence[source, target]
                        part_imag = -part_imag
                    acc_real = (
                        acc_real + part_real * vector_real[source] - part_imag * vector_imag[source]
                    )
                    acc_imag = (
                        acc_imag + part_real * vector_imag[source] + part_imag * vector_real[source]
                    )
            new_real.append(acc_real)
            new_imag.append(acc_imag)
        mean_square = (
            sum(
                (
                    new_real[target] * new_real[target] + new_imag[target] * new_imag[target]
                    for target in range(date_count)
                )
            )
            / date_count
        )
        factor = lax.rsqrt(jnp.maximum(mean_square, 1.0))
        vector_real = [entry * factor for entry in new_real]
        vector_imag = [entry * factor for entry in new_imag]
    magnitude = sum(
        (
            jnp.sqrt(
                coherence[pair][0] * coherence[pair][0] + coherence[pair][1] * coherence[pair][1]
            )
            for pair in pair_list
        )
    ) / len(pair_list)
    quality = valid_mask[:, None] * (0.05 + magnitude)
    vector = jnp.stack([jnp.stack(vector_real), jnp.stack(vector_imag)])
    return (vector, quality)


def shards(raw_echoes, range_phase, azimuth_phase, calibration):
    groups = lax.axis_size("date")
    group_dates = raw_echoes.shape[1]
    local_lines = raw_echoes.shape[2]
    length = raw_echoes.shape[3]
    outer_size = length // 128
    devices = groups * lax.axis_size("strip")
    ranged = range_blocks(raw_echoes.astype(jnp.float32), range_phase)
    tiles = ranged.reshape(devices, -1, 128)
    tiles = lax.all_to_all(tiles, ("date", "strip"), 0, 0, tiled=True)
    strips = devices // groups
    block_range = length // devices
    received = tiles.reshape(groups, strips, block_range, 2, group_dates, local_lines)
    turned = received.transpose(3, 0, 4, 2, 1, 5).reshape(
        2, groups * group_dates, block_range, strips * local_lines
    )
    focused = azimuth_compress(turned, azimuth_phase)
    all_dates = group_dates * groups
    column_count = calibration.shape[1]
    line_count = focused.shape[-1]
    image = focused.reshape(2, all_dates, column_count, line_count) * calibration[None, :, :, None]
    halo = 1 + SMOOTH_PASSES
    axes = ("date", "strip")
    count = lax.axis_size("date") * lax.axis_size("strip")
    up = [(i, i + 1) for i in range(count - 1)]
    edge_shape = (-1, line_count)
    low = lax.ppermute(image[:, :, column_count - halo :].reshape(edge_shape), axes, up)
    high = lax.ppermute(image[:, :, :halo].reshape(edge_shape), axes, [(b, a) for a, b in up])
    total_columns = column_count * lax.axis_size("date") * lax.axis_size("strip")
    first = lax.axis_index(("date", "strip")) * column_count - SMOOTH_PASSES
    columns = first + jnp.arange(column_count + 2 * SMOOTH_PASSES, dtype=jnp.int32)
    valid_mask = ((columns >= 0) & (columns < total_columns)).astype(jnp.float32)
    vector, quality = link_and_smooth((low, image, high), valid_mask)
    return (vector, quality)


def solution(mesh):
    in_specs = (P(None, "date", "strip", None), P(), P(), P(None, ("date", "strip")))
    out_specs = (P(None, None, ("date", "strip"), None), P(("date", "strip"), None))
    return jax.shard_map(shards, mesh=mesh, in_specs=in_specs, out_specs=out_specs, check_vma=False)
```

```python
import functools
import math

import numpy as np

import jax
import jax.numpy as jnp
from jax import lax
from jax.experimental import pallas as pl
from jax.experimental.pallas import tpu as pltpu
from jax.sharding import PartitionSpec as P

WIN_HALF = 11
POWER_ITERS = 6
SMOOTH_PASSES = 2


DFT_PRECISION = lax.Precision.HIGH
BLOCK = 2048
EDGE = 128
CHUNK = 128
ROWS = 8


def link_kernel(column_count, total_columns, band_ref, *refs):
    pieces = refs[:9]
    vec_ref, qual_ref, image, high, low, sums = refs[9:]
    step = pl.program_id(0)
    last = pl.num_programs(0) - 1
    dates = pieces[4].shape[1]
    block = pieces[4].shape[3]
    padded = image.shape[2]
    row = 0
    for number in range(3):
        prev_ref, cur_ref, next_ref = pieces[3 * number : 3 * number + 3]
        if len(cur_ref.shape) == 4:
            count = cur_ref.shape[2]
            rows = slice(row, row + count)
            image[:, :, rows, EDGE : EDGE + block] = cur_ref[...]
            image[:, :, rows, :EDGE] = jnp.where(step > 0, prev_ref[...], 0.0)
            image[:, :, rows, EDGE + block :] = jnp.where(step < last, next_ref[...], 0.0)
        else:
            count = cur_ref.shape[0] // (image.shape[0] * dates)
            rows = slice(row, row + count)
            for p in range(image.shape[0]):
                for d in range(dates):
                    source = slice((p * dates + d) * count, (p * dates + d + 1) * count)
                    image[p, d, rows, EDGE : EDGE + block] = cur_ref[source, :]
                    image[p, d, rows, :EDGE] = jnp.where(step > 0, prev_ref[source, :], 0.0)
                    image[p, d, rows, EDGE + block :] = jnp.where(step < last, next_ref[source, :], 0.0)
        row += count
    image[:, :, row:, :] = jnp.zeros((image.shape[0], dates, padded - row, image.shape[3]), jnp.float32)
    pairs = [(a, b) for a in range(dates) for b in range(a + 1, dates)]
    specs = [(0, a, a) for a in range(dates)]
    for a, b in pairs:
        specs.append((1, a, b))
        specs.append((2, a, b))

    def product(kind, a, b, rows, lanes):
        ra, ia = image[0, a, rows, lanes], image[1, a, rows, lanes]
        if kind == 0:
            return ra * ra + ia * ia
        rb, ib = image[0, b, rows, lanes], image[1, b, rows, lanes]
        if kind == 1:
            return ra * rb + ia * ib
        return ia * rb - ra * ib

    row_index = lax.broadcasted_iota(jnp.int32, (ROWS, CHUNK), 0)

    def term_body(column):
        lanes = slice(column * CHUNK, (column + 1) * CHUNK)
        sums_of_pair = []
        for number, (kind, a, b) in enumerate(specs):
            upper = product(kind, a, b, slice(0, ROWS), lanes)
            lower = product(kind, a, b, slice(ROWS, 2 * ROWS), lanes)
            one = jnp.where(row_index < ROWS - 1, pltpu.roll(upper, ROWS - 1, 0), pltpu.roll(lower, ROWS - 1, 0))
            two = jnp.where(row_index < ROWS - 2, pltpu.roll(upper, ROWS - 2, 0), pltpu.roll(lower, ROWS - 2, 0))
            sums_of_pair.append(upper + one + two)
            if len(sums_of_pair) == 2:
                full = jnp.concatenate(sums_of_pair, axis=0)
                top = full.astype(jnp.bfloat16)
                rows = slice((number - 1) * ROWS, (number + 1) * ROWS)
                high[rows, lanes] = top
                low[rows, lanes] = (full - top.astype(jnp.float32)).astype(jnp.bfloat16)
                sums_of_pair = []

        if column >= 2:
            left = (column - 2) * CHUNK
            window = jnp.dot(high[:, left : left + CHUNK + 2 * EDGE], band, preferred_element_type=jnp.float32)
            window = window + jnp.dot(
                low[:, left : left + CHUNK + 2 * EDGE], band, preferred_element_type=jnp.float32
            )
            sums[:, left : left + CHUNK] = window

    band = band_ref[...]
    for column in range(image.shape[3] // CHUNK):
        term_body(column)
    device = lax.axis_index("date") * lax.axis_size("strip") + lax.axis_index("strip")
    columns = device * column_count - SMOOTH_PASSES + lax.broadcasted_iota(jnp.int32, (ROWS, CHUNK), 0)
    mask = ((columns >= 0) & (columns < total_columns)).astype(jnp.float32)
    inverse_scale = 1.0 / (3 * (2 * WIN_HALF + 1))

    def chunk_body(index, carry):
        start = pl.multiple_of(index * CHUNK, CHUNK)
        window = [
            sums[number * ROWS : (number + 1) * ROWS, pl.ds(start, CHUNK)] * inverse_scale
            for number in range(len(specs))
        ]
        powers = [window[a] + 1e-06 for a in range(dates)]
        coherence = {}
        for number, (a, b) in enumerate(pairs):
            factor = lax.rsqrt(powers[a] * powers[b])
            coherence[a, b] = (
                window[dates + 2 * number] * factor,
                window[dates + 2 * number + 1] * factor,
            )

        def entry(target, source):
            if target < source:
                return coherence[target, source]
            part_real, part_imag = coherence[source, target]
            return part_real, -part_imag

        new_real = []
        new_imag = []
        for target in range(dates):
            sources = [entry(target, source) for source in range(dates) if source != target]
            new_real.append(1.0 + sum(part[0] for part in sources))
            new_imag.append(sum(part[1] for part in sources))
        for iteration in range(POWER_ITERS):
            if iteration > 0:
                new_real = []
                new_imag = []
                for target in range(dates):
                    acc_real = vector_real[target]
                    acc_imag = vector_imag[target]
                    for source in range(dates):
                        if source != target:
                            part_real, part_imag = entry(target, source)
                            acc_real = (
                                acc_real + part_real * vector_real[source] - part_imag * vector_imag[source]
                            )
                            acc_imag = (
                                acc_imag + part_real * vector_imag[source] + part_imag * vector_real[source]
                            )
                    new_real.append(acc_real)
                    new_imag.append(acc_imag)
            mean_square = (
                sum(new_real[t] * new_real[t] + new_imag[t] * new_imag[t] for t in range(dates)) / dates
            )
            factor = lax.rsqrt(jnp.maximum(mean_square, 1.0))
            vector_real = [value * factor for value in new_real]
            vector_imag = [value * factor for value in new_imag]
        magnitude = sum(
            jnp.sqrt(coherence[pair][0] * coherence[pair][0] + coherence[pair][1] * coherence[pair][1])
            for pair in pairs
        ) / len(pairs)
        quality = mask * (0.05 + magnitude)
        vectors = vector_real + vector_imag
        for passes in range(SMOOTH_PASSES):
            denominator = quality + pltpu.roll(quality, 1, 0) + pltpu.roll(quality, ROWS - 1, 0)
            inverse = 1.0 / jnp.where(denominator > 0, denominator, 1.0)
            smoothed = []
            for value in vectors:
                weighted = value * quality
                numerator = weighted + pltpu.roll(weighted, 1, 0) + pltpu.roll(weighted, ROWS - 1, 0)
                smoothed.append(numerator * inverse)
            vectors = smoothed
        keep = slice(SMOOTH_PASSES, ROWS - SMOOTH_PASSES)
        for number, value in enumerate(vectors):
            vec_ref[number // dates, number % dates, :, pl.ds(start, CHUNK)] = value[keep]
        qual_ref[:, pl.ds(start, CHUNK)] = quality[keep]
        return carry

    lax.fori_loop(0, block // CHUNK, chunk_body, 0, unroll=4)


def link_and_smooth(pieces, column_count, total_columns):
    parts, dates, _, lines = pieces[1].shape
    assert all(piece.shape[-1] == lines for piece in pieces)
    padded = 16
    kept = ROWS - 2 * SMOOTH_PASSES
    steps = lines // BLOCK
    per_block = BLOCK // EDGE
    edges = lines // EDGE
    term_count = dates + dates * (dates - 1)
    offset = np.arange(CHUNK + 2 * EDGE)[:, None] - EDGE - np.arange(CHUNK)[None, :]
    band = jnp.asarray(np.abs(offset) <= WIN_HALF, jnp.bfloat16)
    width = BLOCK + 2 * EDGE
    piece_specs = []
    operands = []
    for piece in pieces:
        lead = (0,) * (piece.ndim - 1)
        piece_specs += [
            pl.BlockSpec(piece.shape[:-1] + (EDGE,), lambda i, lead=lead: lead + (jnp.maximum(i * per_block - 1, 0),)),
            pl.BlockSpec(piece.shape[:-1] + (BLOCK,), lambda i, lead=lead: lead + (i,)),
            pl.BlockSpec(piece.shape[:-1] + (EDGE,), lambda i, lead=lead: lead + (jnp.minimum((i + 1) * per_block, edges - 1),)),
        ]
        operands += [piece, piece, piece]
    return pl.pallas_call(
        functools.partial(link_kernel, column_count, total_columns),
        grid=(steps,),
        in_specs=[
            pl.BlockSpec((CHUNK + 2 * EDGE, CHUNK), lambda i: (0, 0)),
        ]
        + piece_specs,
        out_specs=[
            pl.BlockSpec((parts, dates, kept, BLOCK), lambda i: (0, 0, 0, i)),
            pl.BlockSpec((kept, BLOCK), lambda i: (0, i)),
        ],
        out_shape=[
            jax.ShapeDtypeStruct((parts, dates, kept, lines), jnp.float32),
            jax.ShapeDtypeStruct((kept, lines), jnp.float32),
        ],
        scratch_shapes=[
            pltpu.VMEM((parts, dates, padded, width), jnp.float32),
            pltpu.VMEM((term_count * ROWS, width), jnp.bfloat16),
            pltpu.VMEM((term_count * ROWS, width), jnp.bfloat16),
            pltpu.VMEM((term_count * ROWS, BLOCK), jnp.float32),
        ],
    )(band, *operands)


def split_up(x, dim, count):
    shape = x.shape
    tiles = x.reshape(*shape[:dim], count, shape[dim] // count, *shape[dim + 1 :])
    return jnp.moveaxis(tiles, dim, 0)


def laid_out(tiles, dim):
    shape = list(tiles.shape[1:])
    shape[dim] *= tiles.shape[0]
    return jnp.moveaxis(tiles, 0, dim).reshape(shape)


def one_exchange(x, axis, axes, splits, concats):
    sizes = [lax.axis_size(a) for a in axes]
    tiles = split_up(x, splits[0], sizes[0])
    tiles = jnp.moveaxis(split_up(tiles, splits[1] + 1, sizes[1]), 0, 1)
    inside = tiles.shape[2:]
    tiles = tiles.reshape(-1, *inside)
    tiles = lax.all_to_all(tiles, axis, split_axis=0, concat_axis=0, tiled=True)
    tiles = laid_out(tiles.reshape(*sizes, *inside), concats[0] + 1)
    return laid_out(tiles, concats[1])


def extended_2(x, sides, width):
    edges = {}
    for axis, dim in sides:
        count, length = (lax.axis_size(axis), x.shape[dim])
        up = [(i, (i + 1) % count) for i in range(count - 1)]
        last = lax.slice_in_dim(x, length - width, length, axis=dim)
        first = lax.slice_in_dim(x, 0, width, axis=dim)
        edges[dim] = (
            lax.ppermute(last, axis, up),
            lax.ppermute(first, axis, [(b, a) for a, b in up]),
        )
    done = []
    for _, dim in sides:
        low, high = edges[dim]
        around = [(width, width) if d in done else (0, 0) for d in range(x.ndim)]
        x = jnp.concatenate([jnp.pad(low, around), x, jnp.pad(high, around)], axis=dim)
        done.append(dim)
    return x


def dft_table(length, direction):
    counter = jnp.arange(length, dtype=jnp.int32)
    product = counter[:, None] * counter[None, :] % length
    angles = product.astype(jnp.float32) * (direction * 2.0 * math.pi / length)
    cosine = jnp.cos(angles)
    sine_part = jnp.sin(angles)
    return jnp.stack([jnp.stack([cosine, -sine_part]), jnp.stack([sine_part, cosine])])


def twiddle(outer_size, inner_size, direction):
    product = (
        jnp.arange(outer_size, dtype=jnp.int32)[:, None]
        * jnp.arange(inner_size, dtype=jnp.int32)[None, :]
        % (outer_size * inner_size)
    )
    angles = product.astype(jnp.float32) * (direction * 2.0 * math.pi / (outer_size * inner_size))
    return (jnp.cos(angles), jnp.sin(angles))


def rotate(values, cosine, sine_part):
    return jnp.stack(
        [values[0] * cosine - values[1] * sine_part, values[0] * sine_part + values[1] * cosine]
    )


def spectral_core(values, phases):
    outer_size = values.shape[-2]
    inner_size = values.shape[-1]
    values = jnp.einsum("pqkn,q...nm->p...km", dft_table(outer_size, -1), values, precision=DFT_PRECISION)
    cos_part, sin_part = twiddle(outer_size, inner_size, -1)
    values = rotate(values, cos_part, sin_part)
    values = jnp.einsum("pqjm,q...km->p...kj", dft_table(inner_size, -1), values, precision=DFT_PRECISION)
    phase_grid = phases.reshape(inner_size, outer_size).T
    values = rotate(values, jnp.cos(phase_grid), jnp.sin(phase_grid))
    values = jnp.einsum("pqmj,q...kj->p...km", dft_table(inner_size, 1), values, precision=DFT_PRECISION)
    cos_part, sin_part = twiddle(outer_size, inner_size, 1)
    return rotate(values, cos_part, sin_part)


def azimuth_compress(values, phases):
    length = values.shape[-1]
    inner_size = 128
    outer_size = length // inner_size
    spectrum = spectral_core(values.reshape(values.shape[:-1] + (outer_size, inner_size)), phases)
    result = (
        jnp.einsum("pqnk,q...km->p...nm", dft_table(outer_size, 1), spectrum, precision=DFT_PRECISION)
        / length
    )
    return result.reshape(values.shape)


def range_compress(values, phases, row_count):
    length = values.shape[-1]
    inner_size = 128
    outer_size = length // inner_size
    spectrum = spectral_core(values.reshape(values.shape[:-1] + (outer_size, inner_size)), phases)
    inverse_rows = dft_table(outer_size, 1)
    result = jnp.einsum("pqnk,qdlkm->pdnml", inverse_rows, spectrum, precision=DFT_PRECISION) / length
    return result.reshape(2, values.shape[1], row_count * inner_size, values.shape[2])


def range_blocks(values, phases):
    length = values.shape[-1]
    inner_size = 128
    outer_size = length // inner_size
    spectrum = spectral_core(values.reshape(values.shape[:-1] + (outer_size, inner_size)), phases)
    inverse_rows = dft_table(outer_size, 1)
    return jnp.einsum("pqnk,qdlkm->nmpdl", inverse_rows, spectrum, precision=DFT_PRECISION) / length


def running_window(values):
    width = 2 * WIN_HALF + 1
    count = values.shape[-1]
    level = jnp.pad(values, ((0, 0), (0, 0), (WIN_HALF, WIN_HALF)))
    total = jnp.zeros_like(values)
    offset = 0
    span = 1
    while span <= width:
        if width & span:
            total = total + level[..., offset : offset + count]
            offset = offset + span
        level = level[..., :-span] + level[..., span:]
        span = span * 2
    return total


def link_block(real_ext, imag_ext, valid_mask):
    date_count = real_ext.shape[0]
    pair_list = [
        (former, latter) for former in range(date_count) for latter in range(former + 1, date_count)
    ]
    terms = [
        real_ext[former] * real_ext[former] + imag_ext[former] * imag_ext[former]
        for former in range(date_count)
    ]
    for former, latter in pair_list:
        terms.append(real_ext[former] * real_ext[latter] + imag_ext[former] * imag_ext[latter])
        terms.append(imag_ext[former] * real_ext[latter] - real_ext[former] * imag_ext[latter])
    stacked = jnp.stack(terms)
    across = stacked[:, :-2] + stacked[:, 1:-1] + stacked[:, 2:]
    window = running_window(across)
    window = window / (3 * (2 * WIN_HALF + 1))
    powers = window[:date_count] + 1e-06
    coherence = {}
    for number, pair in enumerate(pair_list):
        factor = lax.rsqrt(powers[pair[0]] * powers[pair[1]])
        coherence[pair] = (
            window[date_count + 2 * number] * factor,
            window[date_count + 2 * number + 1] * factor,
        )
    vector_real = [jnp.ones_like(powers[0]) for former in range(date_count)]
    vector_imag = [jnp.zeros_like(powers[0]) for former in range(date_count)]
    for iteration in range(POWER_ITERS):
        new_real = []
        new_imag = []
        for target in range(date_count):
            acc_real = vector_real[target]
            acc_imag = vector_imag[target]
            for source in range(date_count):
                if source != target:
                    if target < source:
                        part_real, part_imag = coherence[target, source]
                    else:
                        part_real, part_imag = coherence[source, target]
                        part_imag = -part_imag
                    acc_real = (
                        acc_real + part_real * vector_real[source] - part_imag * vector_imag[source]
                    )
                    acc_imag = (
                        acc_imag + part_real * vector_imag[source] + part_imag * vector_real[source]
                    )
            new_real.append(acc_real)
            new_imag.append(acc_imag)
        mean_square = (
            sum(
                (
                    new_real[target] * new_real[target] + new_imag[target] * new_imag[target]
                    for target in range(date_count)
                )
            )
            / date_count
        )
        factor = lax.rsqrt(jnp.maximum(mean_square, 1.0))
        vector_real = [entry * factor for entry in new_real]
        vector_imag = [entry * factor for entry in new_imag]
    magnitude = sum(
        (
            jnp.sqrt(
                coherence[pair][0] * coherence[pair][0] + coherence[pair][1] * coherence[pair][1]
            )
            for pair in pair_list
        )
    ) / len(pair_list)
    quality = valid_mask[:, None] * (0.05 + magnitude)
    vector = jnp.stack([jnp.stack(vector_real), jnp.stack(vector_imag)])
    return (vector, quality)


def shards(raw_echoes, range_phase, azimuth_phase, calibration):
    groups = lax.axis_size("date")
    group_dates = raw_echoes.shape[1]
    local_lines = raw_echoes.shape[2]
    length = raw_echoes.shape[3]
    outer_size = length // 128
    devices = groups * lax.axis_size("strip")
    ranged = range_blocks(raw_echoes.astype(jnp.float32), range_phase)
    tiles = ranged.reshape(devices, -1, 128)
    tiles = lax.all_to_all(tiles, ("date", "strip"), 0, 0, tiled=True)
    strips = devices // groups
    block_range = length // devices
    received = tiles.reshape(groups, strips, block_range, 2, group_dates, local_lines)
    turned = received.transpose(3, 0, 4, 2, 1, 5).reshape(
        2, groups * group_dates, block_range, strips * local_lines
    )
    focused = azimuth_compress(turned, azimuth_phase)
    all_dates = group_dates * groups
    column_count = calibration.shape[1]
    line_count = focused.shape[-1]
    image = focused.reshape(2, all_dates, column_count, line_count) * calibration[None, :, :, None]
    halo = 1 + SMOOTH_PASSES
    axes = ("date", "strip")
    count = lax.axis_size("date") * lax.axis_size("strip")
    up = [(i, i + 1) for i in range(count - 1)]
    edge_shape = (-1, line_count)
    low = lax.ppermute(image[:, :, column_count - halo :].reshape(edge_shape), axes, up)
    high = lax.ppermute(image[:, :, :halo].reshape(edge_shape), axes, [(b, a) for a, b in up])
    total_columns = column_count * lax.axis_size("date") * lax.axis_size("strip")
    vector, quality = link_and_smooth((low, image, high), column_count, total_columns)
    return (vector, quality)


def solution(mesh):
    in_specs = (P(None, "date", "strip", None), P(), P(), P(None, ("date", "strip")))
    out_specs = (P(None, None, ("date", "strip"), None), P(("date", "strip"), None))
    return jax.shard_map(shards, mesh=mesh, in_specs=in_specs, out_specs=out_specs, check_vma=False)
```

```python
import functools
import math

import numpy as np

import jax
import jax.numpy as jnp
from jax import lax
from jax.experimental import pallas as pl
from jax.experimental.pallas import tpu as pltpu
from jax.sharding import PartitionSpec as P

WIN_HALF = 11
POWER_ITERS = 6
SMOOTH_PASSES = 2


DFT_PRECISION = lax.Precision.HIGH
BLOCK = 4096
EDGE = 128
CHUNK = 128
ROWS = 8


def link_kernel(column_count, total_columns, band_ref, *refs):
    pieces = refs[:9]
    vec_ref, qual_ref, image, high, low, sums = refs[9:]
    step = pl.program_id(0)
    last = pl.num_programs(0) - 1
    dates = pieces[4].shape[1]
    block = pieces[4].shape[3]
    padded = image.shape[2]
    row = 0
    for number in range(3):
        prev_ref, cur_ref, next_ref = pieces[3 * number : 3 * number + 3]
        if len(cur_ref.shape) == 4:
            count = cur_ref.shape[2]
            rows = slice(row, row + count)
            image[:, :, rows, EDGE : EDGE + block] = cur_ref[...]
            image[:, :, rows, :EDGE] = jnp.where(step > 0, prev_ref[...], 0.0)
            image[:, :, rows, EDGE + block :] = jnp.where(step < last, next_ref[...], 0.0)
        else:
            count = cur_ref.shape[0] // (image.shape[0] * dates)
            rows = slice(row, row + count)
            for p in range(image.shape[0]):
                for d in range(dates):
                    source = slice((p * dates + d) * count, (p * dates + d + 1) * count)
                    image[p, d, rows, EDGE : EDGE + block] = cur_ref[source, :]
                    image[p, d, rows, :EDGE] = jnp.where(step > 0, prev_ref[source, :], 0.0)
                    image[p, d, rows, EDGE + block :] = jnp.where(step < last, next_ref[source, :], 0.0)
        row += count
    image[:, :, row:, :] = jnp.zeros((image.shape[0], dates, padded - row, image.shape[3]), jnp.float32)
    pairs = [(a, b) for a in range(dates) for b in range(a + 1, dates)]
    specs = [(0, a, a) for a in range(dates)]
    for a, b in pairs:
        specs.append((1, a, b))
        specs.append((2, a, b))

    def product(kind, a, b, rows, lanes):
        ra, ia = image[0, a, rows, lanes], image[1, a, rows, lanes]
        if kind == 0:
            return ra * ra + ia * ia
        rb, ib = image[0, b, rows, lanes], image[1, b, rows, lanes]
        if kind == 1:
            return ra * rb + ia * ib
        return ia * rb - ra * ib

    row_index = lax.broadcasted_iota(jnp.int32, (ROWS, CHUNK), 0)

    def term_body(column):
        lanes = slice(column * CHUNK, (column + 1) * CHUNK)
        sums_of_pair = []
        for number, (kind, a, b) in enumerate(specs):
            upper = product(kind, a, b, slice(0, ROWS), lanes)
            lower = product(kind, a, b, slice(ROWS, 2 * ROWS), lanes)
            one = jnp.where(row_index < ROWS - 1, pltpu.roll(upper, ROWS - 1, 0), pltpu.roll(lower, ROWS - 1, 0))
            two = jnp.where(row_index < ROWS - 2, pltpu.roll(upper, ROWS - 2, 0), pltpu.roll(lower, ROWS - 2, 0))
            sums_of_pair.append(upper + one + two)
            if len(sums_of_pair) == 2:
                full = jnp.concatenate(sums_of_pair, axis=0)
                top = full.astype(jnp.bfloat16)
                rows = slice((number - 1) * ROWS, (number + 1) * ROWS)
                high[rows, lanes] = top
                low[rows, lanes] = (full - top.astype(jnp.float32)).astype(jnp.bfloat16)
                sums_of_pair = []

        if column >= 2:
            left = (column - 2) * CHUNK
            window = jnp.dot(high[:, left : left + CHUNK + 2 * EDGE], band, preferred_element_type=jnp.float32)
            window = window + jnp.dot(
                low[:, left : left + CHUNK + 2 * EDGE], band, preferred_element_type=jnp.float32
            )
            sums[:, left : left + CHUNK] = window

    band = band_ref[...]
    for column in range(image.shape[3] // CHUNK):
        term_body(column)
    device = lax.axis_index("date") * lax.axis_size("strip") + lax.axis_index("strip")
    columns = device * column_count - SMOOTH_PASSES + lax.broadcasted_iota(jnp.int32, (ROWS, CHUNK), 0)
    mask = ((columns >= 0) & (columns < total_columns)).astype(jnp.float32)
    inverse_scale = 1.0 / (3 * (2 * WIN_HALF + 1))

    def chunk_body(index, carry):
        start = pl.multiple_of(index * CHUNK, CHUNK)
        window = [sums[number * ROWS : (number + 1) * ROWS, pl.ds(start, CHUNK)] for number in range(len(specs))]
        powers = [window[a] * inverse_scale + 1e-06 for a in range(dates)]
        coherence = {}
        for number, (a, b) in enumerate(pairs):
            factor = lax.rsqrt(powers[a] * powers[b]) * inverse_scale
            coherence[a, b] = (
                window[dates + 2 * number] * factor,
                window[dates + 2 * number + 1] * factor,
            )

        def entry(target, source):
            if target < source:
                return coherence[target, source]
            part_real, part_imag = coherence[source, target]
            return part_real, -part_imag

        new_real = []
        new_imag = []
        for target in range(dates):
            sources = [entry(target, source) for source in range(dates) if source != target]
            new_real.append(1.0 + sum(part[0] for part in sources))
            new_imag.append(sum(part[1] for part in sources))
        for iteration in range(POWER_ITERS):
            if iteration > 0:
                new_real = []
                new_imag = []
                for target in range(dates):
                    acc_real = vector_real[target]
                    acc_imag = vector_imag[target]
                    for source in range(dates):
                        if source != target:
                            part_real, part_imag = entry(target, source)
                            acc_real = (
                                acc_real + part_real * vector_real[source] - part_imag * vector_imag[source]
                            )
                            acc_imag = (
                                acc_imag + part_real * vector_imag[source] + part_imag * vector_real[source]
                            )
                    new_real.append(acc_real)
                    new_imag.append(acc_imag)
            mean_square = (
                sum(new_real[t] * new_real[t] + new_imag[t] * new_imag[t] for t in range(dates)) / dates
            )
            factor = lax.rsqrt(jnp.maximum(mean_square, 1.0))
            vector_real = [value * factor for value in new_real]
            vector_imag = [value * factor for value in new_imag]
        magnitude = sum(
            jnp.sqrt(coherence[pair][0] * coherence[pair][0] + coherence[pair][1] * coherence[pair][1])
            for pair in pairs
        ) / len(pairs)
        quality = mask * (0.05 + magnitude)
        vectors = vector_real + vector_imag
        for passes in range(SMOOTH_PASSES):
            denominator = quality + pltpu.roll(quality, 1, 0) + pltpu.roll(quality, ROWS - 1, 0)
            inverse = 1.0 / jnp.where(denominator > 0, denominator, 1.0)
            smoothed = []
            for value in vectors:
                weighted = value * quality
                numerator = weighted + pltpu.roll(weighted, 1, 0) + pltpu.roll(weighted, ROWS - 1, 0)
                smoothed.append(numerator * inverse)
            vectors = smoothed
        keep = slice(SMOOTH_PASSES, ROWS - SMOOTH_PASSES)
        for number, value in enumerate(vectors):
            vec_ref[number // dates, number % dates, :, pl.ds(start, CHUNK)] = value[keep]
        qual_ref[:, pl.ds(start, CHUNK)] = quality[keep]
        return carry

    lax.fori_loop(0, block // CHUNK, chunk_body, 0, unroll=4)


def link_and_smooth(pieces, column_count, total_columns):
    parts, dates, _, lines = pieces[1].shape
    assert all(piece.shape[-1] == lines for piece in pieces)
    padded = 16
    kept = ROWS - 2 * SMOOTH_PASSES
    steps = lines // BLOCK
    per_block = BLOCK // EDGE
    edges = lines // EDGE
    term_count = dates + dates * (dates - 1)
    offset = np.arange(CHUNK + 2 * EDGE)[:, None] - EDGE - np.arange(CHUNK)[None, :]
    band = jnp.asarray(np.abs(offset) <= WIN_HALF, jnp.bfloat16)
    width = BLOCK + 2 * EDGE
    piece_specs = []
    operands = []
    for piece in pieces:
        lead = (0,) * (piece.ndim - 1)
        piece_specs += [
            pl.BlockSpec(piece.shape[:-1] + (EDGE,), lambda i, lead=lead: lead + (jnp.maximum(i * per_block - 1, 0),)),
            pl.BlockSpec(piece.shape[:-1] + (BLOCK,), lambda i, lead=lead: lead + (i,)),
            pl.BlockSpec(piece.shape[:-1] + (EDGE,), lambda i, lead=lead: lead + (jnp.minimum((i + 1) * per_block, edges - 1),)),
        ]
        operands += [piece, piece, piece]
    return pl.pallas_call(
        functools.partial(link_kernel, column_count, total_columns),
        grid=(steps,),
        in_specs=[
            pl.BlockSpec((CHUNK + 2 * EDGE, CHUNK), lambda i: (0, 0)),
        ]
        + piece_specs,
        out_specs=[
            pl.BlockSpec((parts, dates, kept, BLOCK), lambda i: (0, 0, 0, i)),
            pl.BlockSpec((kept, BLOCK), lambda i: (0, i)),
        ],
        out_shape=[
            jax.ShapeDtypeStruct((parts, dates, kept, lines), jnp.float32),
            jax.ShapeDtypeStruct((kept, lines), jnp.float32),
        ],
        scratch_shapes=[
            pltpu.VMEM((parts, dates, padded, width), jnp.float32),
            pltpu.VMEM((term_count * ROWS, width), jnp.bfloat16),
            pltpu.VMEM((term_count * ROWS, width), jnp.bfloat16),
            pltpu.VMEM((term_count * ROWS, BLOCK), jnp.float32),
        ],
    )(band, *operands)


def split_up(x, dim, count):
    shape = x.shape
    tiles = x.reshape(*shape[:dim], count, shape[dim] // count, *shape[dim + 1 :])
    return jnp.moveaxis(tiles, dim, 0)


def laid_out(tiles, dim):
    shape = list(tiles.shape[1:])
    shape[dim] *= tiles.shape[0]
    return jnp.moveaxis(tiles, 0, dim).reshape(shape)


def one_exchange(x, axis, axes, splits, concats):
    sizes = [lax.axis_size(a) for a in axes]
    tiles = split_up(x, splits[0], sizes[0])
    tiles = jnp.moveaxis(split_up(tiles, splits[1] + 1, sizes[1]), 0, 1)
    inside = tiles.shape[2:]
    tiles = tiles.reshape(-1, *inside)
    tiles = lax.all_to_all(tiles, axis, split_axis=0, concat_axis=0, tiled=True)
    tiles = laid_out(tiles.reshape(*sizes, *inside), concats[0] + 1)
    return laid_out(tiles, concats[1])


def extended_2(x, sides, width):
    edges = {}
    for axis, dim in sides:
        count, length = (lax.axis_size(axis), x.shape[dim])
        up = [(i, (i + 1) % count) for i in range(count - 1)]
        last = lax.slice_in_dim(x, length - width, length, axis=dim)
        first = lax.slice_in_dim(x, 0, width, axis=dim)
        edges[dim] = (
            lax.ppermute(last, axis, up),
            lax.ppermute(first, axis, [(b, a) for a, b in up]),
        )
    done = []
    for _, dim in sides:
        low, high = edges[dim]
        around = [(width, width) if d in done else (0, 0) for d in range(x.ndim)]
        x = jnp.concatenate([jnp.pad(low, around), x, jnp.pad(high, around)], axis=dim)
        done.append(dim)
    return x


def dft_table(length, direction):
    counter = jnp.arange(length, dtype=jnp.int32)
    product = counter[:, None] * counter[None, :] % length
    angles = product.astype(jnp.float32) * (direction * 2.0 * math.pi / length)
    cosine = jnp.cos(angles)
    sine_part = jnp.sin(angles)
    return jnp.stack([jnp.stack([cosine, -sine_part]), jnp.stack([sine_part, cosine])])


def twiddle(outer_size, inner_size, direction):
    product = (
        jnp.arange(outer_size, dtype=jnp.int32)[:, None]
        * jnp.arange(inner_size, dtype=jnp.int32)[None, :]
        % (outer_size * inner_size)
    )
    angles = product.astype(jnp.float32) * (direction * 2.0 * math.pi / (outer_size * inner_size))
    return (jnp.cos(angles), jnp.sin(angles))


def rotate(values, cosine, sine_part):
    return jnp.stack(
        [values[0] * cosine - values[1] * sine_part, values[0] * sine_part + values[1] * cosine]
    )


def spectral_core(values, phases):
    outer_size = values.shape[-2]
    inner_size = values.shape[-1]
    values = jnp.einsum("pqkn,q...nm->p...km", dft_table(outer_size, -1), values, precision=DFT_PRECISION)
    cos_part, sin_part = twiddle(outer_size, inner_size, -1)
    values = rotate(values, cos_part, sin_part)
    values = jnp.einsum("pqjm,q...km->p...kj", dft_table(inner_size, -1), values, precision=DFT_PRECISION)
    phase_grid = phases.reshape(inner_size, outer_size).T
    values = rotate(values, jnp.cos(phase_grid), jnp.sin(phase_grid))
    values = jnp.einsum("pqmj,q...kj->p...km", dft_table(inner_size, 1), values, precision=DFT_PRECISION)
    cos_part, sin_part = twiddle(outer_size, inner_size, 1)
    return rotate(values, cos_part, sin_part)


def azimuth_compress(values, phases):
    length = values.shape[-1]
    inner_size = 128
    outer_size = length // inner_size
    spectrum = spectral_core(values.reshape(values.shape[:-1] + (outer_size, inner_size)), phases)
    result = (
        jnp.einsum("pqnk,q...km->p...nm", dft_table(outer_size, 1), spectrum, precision=DFT_PRECISION)
        / length
    )
    return result.reshape(values.shape)


def range_compress(values, phases, row_count):
    length = values.shape[-1]
    inner_size = 128
    outer_size = length // inner_size
    spectrum = spectral_core(values.reshape(values.shape[:-1] + (outer_size, inner_size)), phases)
    inverse_rows = dft_table(outer_size, 1)
    result = jnp.einsum("pqnk,qdlkm->pdnml", inverse_rows, spectrum, precision=DFT_PRECISION) / length
    return result.reshape(2, values.shape[1], row_count * inner_size, values.shape[2])


def range_blocks(values, phases):
    length = values.shape[-1]
    inner_size = 128
    outer_size = length // inner_size
    spectrum = spectral_core(values.reshape(values.shape[:-1] + (outer_size, inner_size)), phases)
    inverse_rows = dft_table(outer_size, 1)
    return jnp.einsum("pqnk,qdlkm->nmpdl", inverse_rows, spectrum, precision=DFT_PRECISION) / length


def running_window(values):
    width = 2 * WIN_HALF + 1
    count = values.shape[-1]
    level = jnp.pad(values, ((0, 0), (0, 0), (WIN_HALF, WIN_HALF)))
    total = jnp.zeros_like(values)
    offset = 0
    span = 1
    while span <= width:
        if width & span:
            total = total + level[..., offset : offset + count]
            offset = offset + span
        level = level[..., :-span] + level[..., span:]
        span = span * 2
    return total


def link_block(real_ext, imag_ext, valid_mask):
    date_count = real_ext.shape[0]
    pair_list = [
        (former, latter) for former in range(date_count) for latter in range(former + 1, date_count)
    ]
    terms = [
        real_ext[former] * real_ext[former] + imag_ext[former] * imag_ext[former]
        for former in range(date_count)
    ]
    for former, latter in pair_list:
        terms.append(real_ext[former] * real_ext[latter] + imag_ext[former] * imag_ext[latter])
        terms.append(imag_ext[former] * real_ext[latter] - real_ext[former] * imag_ext[latter])
    stacked = jnp.stack(terms)
    across = stacked[:, :-2] + stacked[:, 1:-1] + stacked[:, 2:]
    window = running_window(across)
    window = window / (3 * (2 * WIN_HALF + 1))
    powers = window[:date_count] + 1e-06
    coherence = {}
    for number, pair in enumerate(pair_list):
        factor = lax.rsqrt(powers[pair[0]] * powers[pair[1]])
        coherence[pair] = (
            window[date_count + 2 * number] * factor,
            window[date_count + 2 * number + 1] * factor,
        )
    vector_real = [jnp.ones_like(powers[0]) for former in range(date_count)]
    vector_imag = [jnp.zeros_like(powers[0]) for former in range(date_count)]
    for iteration in range(POWER_ITERS):
        new_real = []
        new_imag = []
        for target in range(date_count):
            acc_real = vector_real[target]
            acc_imag = vector_imag[target]
            for source in range(date_count):
                if source != target:
                    if target < source:
                        part_real, part_imag = coherence[target, source]
                    else:
                        part_real, part_imag = coherence[source, target]
                        part_imag = -part_imag
                    acc_real = (
                        acc_real + part_real * vector_real[source] - part_imag * vector_imag[source]
                    )
                    acc_imag = (
                        acc_imag + part_real * vector_imag[source] + part_imag * vector_real[source]
                    )
            new_real.append(acc_real)
            new_imag.append(acc_imag)
        mean_square = (
            sum(
                (
                    new_real[target] * new_real[target] + new_imag[target] * new_imag[target]
                    for target in range(date_count)
                )
            )
            / date_count
        )
        factor = lax.rsqrt(jnp.maximum(mean_square, 1.0))
        vector_real = [entry * factor for entry in new_real]
        vector_imag = [entry * factor for entry in new_imag]
    magnitude = sum(
        (
            jnp.sqrt(
                coherence[pair][0] * coherence[pair][0] + coherence[pair][1] * coherence[pair][1]
            )
            for pair in pair_list
        )
    ) / len(pair_list)
    quality = valid_mask[:, None] * (0.05 + magnitude)
    vector = jnp.stack([jnp.stack(vector_real), jnp.stack(vector_imag)])
    return (vector, quality)


def shards(raw_echoes, range_phase, azimuth_phase, calibration):
    groups = lax.axis_size("date")
    group_dates = raw_echoes.shape[1]
    local_lines = raw_echoes.shape[2]
    length = raw_echoes.shape[3]
    outer_size = length // 128
    devices = groups * lax.axis_size("strip")
    ranged = range_blocks(raw_echoes.astype(jnp.float32), range_phase)
    tiles = ranged.reshape(devices, -1, 128)
    tiles = lax.all_to_all(tiles, ("date", "strip"), 0, 0, tiled=True)
    strips = devices // groups
    block_range = length // devices
    received = tiles.reshape(groups, strips, block_range, 2, group_dates, local_lines)
    turned = received.transpose(3, 0, 4, 2, 1, 5).reshape(
        2, groups * group_dates, block_range, strips * local_lines
    )
    focused = azimuth_compress(turned, azimuth_phase)
    all_dates = group_dates * groups
    column_count = calibration.shape[1]
    line_count = focused.shape[-1]
    image = focused.reshape(2, all_dates, column_count, line_count) * calibration[None, :, :, None]
    halo = 1 + SMOOTH_PASSES
    axes = ("date", "strip")
    count = lax.axis_size("date") * lax.axis_size("strip")
    up = [(i, i + 1) for i in range(count - 1)]
    edge_shape = (-1, line_count)
    low = lax.ppermute(image[:, :, column_count - halo :].reshape(edge_shape), axes, up)
    high = lax.ppermute(image[:, :, :halo].reshape(edge_shape), axes, [(b, a) for a, b in up])
    total_columns = column_count * lax.axis_size("date") * lax.axis_size("strip")
    vector, quality = link_and_smooth((low, image, high), column_count, total_columns)
    return (vector, quality)


def solution(mesh):
    in_specs = (P(None, "date", "strip", None), P(), P(), P(None, ("date", "strip")))
    out_specs = (P(None, None, ("date", "strip"), None), P(("date", "strip"), None))
    return jax.shard_map(shards, mesh=mesh, in_specs=in_specs, out_specs=out_specs, check_vma=False)
```
